32 devices in a mesh: grp: 4 (over y, x), sta: 8 (over z, core).
Axes of the slice: x: 2, y: 2, z: 4, core: 2. Of those that a mesh axis runs over, the one named last changes fastest.
Arguments:
- spectra: float32 [256, 2, 18432], P(('grp', 'sta')), may hold values from -61 to 61
- stacks: float32 [3072, 1601], P(('grp', 'sta')), may hold values from -6 to 6
- pair_sta: int32 [2, 3072], P(None, ('grp', 'sta')), may hold values from 0 to 63
- pair_valid: int32 [3072], P(('grp', 'sta')), may hold values 0 or 1
- owner: int32 [3072, 1], P(('grp', 'sta')), may hold values from 0 to 31; in each aligned block of 96 rows (0 to 95, 96 to 191, ...) at most 4 rows name the same one
- slot: int32 [3072], P(('grp', 'sta')), may hold values from 0 to 95
Outputs:
- stacks_new: float32 [3072, 1601], P(('grp', 'sta'))
The draws below stay inside these ranges and needn't reach their ends.
Inputs may be any that keep to these rules, and one draw needn't show every extreme that they name: Among the 96 rows of one device no owner is named more than 4 times.
All inputs are finite; a program needn't handle non-finite values. No bound on the sum of `pair_valid` on one device may be relied on, other than what follows from the above.
Results may differ from the reference program's by a relative error of at most 0.0041.
Values may be sent and summed in bfloat16 or wider, within the bound.
No kernel may reach another device: no remote copies, remote signals or barrier semaphores. Data moves between devices by JAX's collectives and lax.ppermute only.
A program may use at most 128 MiB of HBM per device.

```python
import math
import jax
import jax.numpy as jnp
import numpy as np
from jax import lax

F = 18432
BAND = 64
LAGS = 1601
P_DEV = 96
CAP = 4
STK_DEV = 96
GSTA = 64
STATIONS = 256
PAIRS = 3072
STACKS = 3072
N_STA = 8
DEVICES = 32


def draw_spectra(key, part):
    key_base, key_scale = jax.random.split(jax.random.fold_in(key, 17))
    base = jnp.clip(jax.random.normal(key_base, (STATIONS, 2, F // BAND, BAND), jnp.float32), -5.0, 5.0)
    level = jax.random.uniform(key_scale, (STATIONS, 1, F // BAND, 1), jnp.float32, -1.5, 1.5)
    return (base * jnp.exp(level)).reshape(STATIONS, 2, F)


def plant(values, key, least, largest):
    longest = values.shape.index(max(values.shape))
    spots = []
    for shift in (0, 1):
        where = [jax.random.randint(jax.random.fold_in(key, axis), (), 0, length) for axis, length in enumerate(values.shape)]
        where[longest] = (where[longest] + shift) % values.shape[longest]
        spots.append(tuple(where))
    return values.at[spots[0]].set(least).at[spots[1]].set(largest)


def levels(own_key, shape, shards, low, largest):
    def one(dim, blocks):
        heights = jax.random.uniform(jax.random.fold_in(jax.random.fold_in(own_key, 6), dim), (blocks,), jnp.float32, low / len(shards), largest / len(shards))
        return jnp.repeat(jnp.exp(heights), shape[dim] // blocks).reshape((-1,) + (1,) * (len(shape) - dim - 1))

    loudness = one(*shards[0])
    for cut in shards[1:]:
        loudness = loudness * one(*cut)
    return loudness


def routed_block(stream_key, own, number, rows, amount, top, most, lean):
    ranking = jax.random.permutation(stream_key, amount)
    heavy_load, ordinary = shares(amount, rows * top, most, lean, True), shares(amount, rows * top, most, lean, False)
    places = jnp.arange(amount)

    def named(tallies, turn):
        used = int((tallies > 0).sum())
        fixed = max(1, used // 4)
        shifted = fixed + (places - fixed + turn * (used - fixed)) % max(1, amount - fixed)
        return jnp.zeros((amount,), jnp.int32).at[ranking[jnp.where(places < fixed, places, shifted)]].set(jnp.asarray(tallies, jnp.int32))

    tallies = jnp.where(number % 4 == 0, named(heavy_load, number // 4), named(ordinary, number - number // 4 - 1))
    mixed = jax.random.permutation(jax.random.fold_in(own, 3), amount)
    donor, taker = mixed[0:amount // 2 * 2:2], mixed[1:amount // 2 * 2:2]
    margin = jnp.minimum(tallies[donor] - 1, most - tallies[taker]) // 2
    margin = jnp.where((donor == ranking[0]) | (taker == ranking[0]) | (tallies[taker] == 0), 0, jnp.maximum(margin, 0))
    shifted = jax.random.randint(jax.random.fold_in(own, 4), (amount // 2,), 0, 1 << 20) % (margin + 1)
    tallies = tallies.at[donor].add(-shifted).at[taker].add(shifted)
    labels = jnp.searchsorted(jnp.cumsum(tallies), jnp.arange(rows * top), side="right").astype(jnp.int32)
    table = labels.reshape(top, rows).T
    table = table[jax.random.permutation(jax.random.fold_in(own, 1), rows)]
    turn = jax.random.randint(jax.random.fold_in(own, 2), (rows, 1), 0, top)
    return jnp.take_along_axis(table, (jnp.arange(top)[None, :] + turn) % top, axis=1)


def shares(number_of, total, limit, skew, full):
    portions = [(1 << 20) // math.isqrt(standing ** skew) + 1 for standing in range(1, number_of + 1)]
    largest = limit if full else min(limit, max(-(-total // number_of), total * portions[0] // sum(portions)))
    least = 1 if total - largest >= number_of - 1 else 0
    counts, spare = [largest] + [least] * (number_of - 1), total - largest - least * (number_of - 1)
    while spare > 0:
        movable = [i for i in range(1, number_of) if counts[i] < largest] or [i for i in range(1, number_of) if counts[i] < limit]
        pool, left = sum([portions[i] for i in movable]), spare
        for i in movable:
            addition = min(limit - counts[i], max(1, left * portions[i] // pool), spare)
            counts[i] = counts[i] + addition
            spare = spare - addition
    return np.array(counts)


def centred(key, shape, scale, limit, shards=(), kind=jnp.bfloat16):
    result = scale * jax.random.normal(key, shape, jnp.float32)
    if shards:
        result = result * levels(key, shape, shards, -0.22, 0.18)
    return jnp.clip(result, -limit, limit).astype(kind)


def setup_inputs(seed: int = 0) -> dict:
    splits = jax.random.split(jax.random.key(seed), 7)
    spectra = draw_spectra(jax.random.fold_in(splits[6], 71), 0)
    stacks = centred(splits[1], (STACKS, LAGS), 1.0, 6.0, ((0, 32),), jnp.float32)
    pair_sta = plant(jax.random.randint(splits[2], (2, PAIRS), 0, GSTA), jax.random.fold_in(splits[2], 1), 0, GSTA - 1).astype(jnp.int32)
    pair_valid = plant((jax.random.randint(splits[3], (PAIRS,), 0, 4) < 3).astype(jnp.int32), jax.random.fold_in(splits[3], 1), 0, 1)
    owner_keys = jax.random.split(jax.random.fold_in(splits[4], 1), PAIRS // P_DEV)
    owner_turns = jax.random.permutation(jax.random.fold_in(splits[4], 3), PAIRS // P_DEV)
    owner = jax.vmap(lambda own, number: routed_block(jax.random.fold_in(splits[4], 2), own, number, P_DEV, DEVICES, 1, CAP, 2))(owner_keys, owner_turns).reshape((PAIRS, 1))
    slot = plant(jax.random.randint(splits[5], (PAIRS,), 0, STK_DEV), jax.random.fold_in(splits[5], 1), 0, STK_DEV - 1).astype(jnp.int32)
    return {"spectra": spectra, "stacks": stacks, "pair_sta": pair_sta, "pair_valid": pair_valid, "owner": owner, "slot": slot}


def whiten(spectra):
    shape = spectra.shape
    split = spectra.reshape(shape[0], 2, shape[2] // BAND, BAND)
    power = lax.optimization_barrier(jnp.mean(split * split, axis=(1, 3), keepdims=True))
    return (split * lax.rsqrt(power + 1e-06)).reshape(shape).astype(jnp.bfloat16)

def lag_table():
    freqs = jnp.arange(F, dtype=jnp.int32)
    shifts = jnp.arange(LAGS, dtype=jnp.int32) - (LAGS - 1) // 2
    angle_ids = jnp.mod(freqs[:, None] * shifts[None, :], 2 * F).astype(jnp.int32)
    theta = angle_ids.astype(jnp.float32) * jnp.float32(math.pi / F)
    return jnp.concatenate([jnp.cos(theta), -jnp.sin(theta)], axis=0).astype(jnp.bfloat16)

def reference(spectra, stacks, pair_sta, pair_valid, owner, slot):
    whitened = whiten(spectra)
    table = lag_table()
    groups = (jnp.arange(PAIRS, dtype=jnp.int32) // (P_DEV * N_STA)).astype(jnp.int32)
    first_ids = (groups * GSTA + pair_sta[0]).astype(jnp.int32).reshape(DEVICES, P_DEV)
    second_ids = (groups * GSTA + pair_sta[1]).astype(jnp.int32).reshape(DEVICES, P_DEV)

    def one_block(ids):
        first = whitened[ids[0]].astype(jnp.float32)
        second = whitened[ids[1]].astype(jnp.float32)
        real_part = first[:, 0] * second[:, 0] + first[:, 1] * second[:, 1]
        imag_part = first[:, 1] * second[:, 0] - first[:, 0] * second[:, 1]
        cross = jnp.concatenate([real_part, imag_part], axis=1).astype(jnp.bfloat16)
        return jnp.dot(cross, table, preferred_element_type=jnp.float32)
    corr = lax.map(one_block, (first_ids, second_ids)).reshape(PAIRS, LAGS)
    corr = corr * jnp.float32(F ** (-0.5)) * pair_valid.astype(jnp.float32)[:, None]
    targets = (owner[:, 0] * STK_DEV + slot).astype(jnp.int32)
    return stacks + jnp.zeros_like(stacks).at[targets].add(corr)
```

```python
import math

import jax
import jax.numpy as jnp
from jax import lax
from jax.sharding import PartitionSpec as P

BAND = 64


def whiten(spectra):
    shape = spectra.shape
    split = spectra.reshape(shape[0], 2, shape[2] // BAND, BAND)
    power = jnp.mean(split * split, axis=(1, 3), keepdims=True)
    return (split * lax.rsqrt(power + 1e-06)).reshape(shape).astype(jnp.bfloat16)


def angle_table(freqs, lag_count, total_bins):
    shifts = lax.iota(jnp.int32, lag_count) - (lag_count - 1) // 2
    angle_ids = jnp.mod(freqs[:, None] * shifts[None, :], 2 * total_bins)
    theta = angle_ids.astype(jnp.float32) * jnp.float32(math.pi / total_bins)
    return jnp.cos(theta), jnp.sin(theta)


def local(spectra, stacks, pair_sta, pair_valid, owner, slot):
    total_bins = spectra.shape[2]
    lag_count = stacks.shape[1]
    stack_rows = stacks.shape[0]
    pair_count = pair_sta.shape[1]
    groups = lax.axis_size("grp")
    members = lax.axis_size("sta")
    devices = groups * members
    capacity = max(2, (4 * pair_count + 3 * devices - 1) // (3 * devices))
    whitened = whiten(spectra)
    gathered = lax.all_gather(whitened, "sta", axis=0, tiled=True)
    group_sta = gathered.shape[0]
    flat = gathered.reshape(group_sta, 2 * total_bins)
    sta_ids = lax.iota(jnp.int32, group_sta)[None, :]
    pick0 = (pair_sta[0][:, None] == sta_ids).astype(jnp.bfloat16)
    pick1 = (pair_sta[1][:, None] == sta_ids).astype(jnp.bfloat16)
    first = jnp.dot(pick0, flat, preferred_element_type=jnp.float32).reshape(pair_count, 2, total_bins)
    second = jnp.dot(pick1, flat, preferred_element_type=jnp.float32).reshape(pair_count, 2, total_bins)
    real_all = (first[:, 0] * second[:, 0] + first[:, 1] * second[:, 1]).astype(jnp.bfloat16)
    imag_all = (first[:, 1] * second[:, 0] - first[:, 0] * second[:, 1]).astype(jnp.bfloat16)

    low = 64
    fblock = 2048
    assert total_bins % fblock == 0 and fblock % low == 0
    hi_count = fblock // low
    cos_hi, sin_hi = angle_table(lax.iota(jnp.int32, total_bins // low) * low, lag_count, total_bins)
    cos_lo, sin_lo = angle_table(lax.iota(jnp.int32, low), lag_count, total_bins)

    def add_block(index, total):
        start = index * fblock
        left = lax.dynamic_slice_in_dim(real_all, start, fblock, 1)
        right = lax.dynamic_slice_in_dim(imag_all, start, fblock, 1)
        ch = lax.dynamic_slice_in_dim(cos_hi, index * hi_count, hi_count, 0)[:, None, :]
        sh = lax.dynamic_slice_in_dim(sin_hi, index * hi_count, hi_count, 0)[:, None, :]
        cosines = (ch * cos_lo[None] - sh * sin_lo[None]).reshape(fblock, lag_count)
        sines = (-(sh * cos_lo[None] + ch * sin_lo[None])).reshape(fblock, lag_count)
        total = total + jnp.dot(left, cosines.astype(jnp.bfloat16), preferred_element_type=jnp.float32)
        return total + jnp.dot(right, sines.astype(jnp.bfloat16), preferred_element_type=jnp.float32)

    corr = lax.fori_loop(
        0, total_bins // fblock, add_block, jnp.zeros((pair_count, lag_count), jnp.float32)
    )
    corr = corr * jnp.float32(total_bins ** (-0.5)) * pair_valid.astype(jnp.float32)[:, None]
    dest = owner[:, 0]
    dest_hot = (dest[:, None] == lax.iota(jnp.int32, devices)[None, :]).astype(jnp.int32)
    before = jnp.cumsum(dest_hot, axis=0) - dest_hot
    position = jnp.sum(before * dest_hot, axis=1)
    flat = dest * capacity + position
    placing = (flat[:, None] == lax.iota(jnp.int32, devices * capacity)[None, :]).astype(
        jnp.float32
    )
    send_rows = jnp.dot(placing.T, corr, precision=lax.Precision.HIGHEST)
    send_slots = jnp.dot(
        placing.T, slot.astype(jnp.float32)[:, None], precision=lax.Precision.HIGHEST
    )[:, 0]
    got_rows, got_slots = (
        lax.all_to_all(
            send_rows.reshape(devices, capacity, lag_count),
            ("grp", "sta"),
            split_axis=0,
            concat_axis=0,
            tiled=True,
        ),
        lax.all_to_all(
            send_slots.reshape(devices, capacity),
            ("grp", "sta"),
            split_axis=0,
            concat_axis=0,
            tiled=True,
        ),
    )
    got_rows = got_rows.reshape(devices * capacity, lag_count)
    got_slots = got_slots.reshape(devices * capacity)
    adding = (
        got_slots[None, :] == lax.iota(jnp.int32, stack_rows).astype(jnp.float32)[:, None]
    ).astype(jnp.float32)
    return stacks + jnp.dot(adding, got_rows, precision=lax.Precision.HIGHEST)


def solution(mesh):
    return jax.shard_map(
        local,
        mesh=mesh,
        in_specs=(
            P(("grp", "sta"), None, None),
            P(("grp", "sta"), None),
            P(None, ("grp", "sta")),
            P(("grp", "sta")),
            P(("grp", "sta"), None),
            P(("grp", "sta")),
        ),
        out_specs=P(("grp", "sta"), None),
        check_vma=False,
    )
```

```python
import math

import jax
import jax.numpy as jnp
from jax import lax
from jax.experimental import pallas as pl
from jax.experimental.pallas import tpu as pltpu
from jax.sharding import PartitionSpec as P

BAND = 64


def whiten(spectra):
    shape = spectra.shape
    split = spectra.reshape(shape[0], 2, shape[2] // BAND, BAND)
    power = jnp.mean(split * split, axis=(1, 3), keepdims=True)
    return (split * lax.rsqrt(power + 1e-06)).reshape(shape).astype(jnp.bfloat16)


def angle_table(freqs, lag_pad, lag_count, total_bins):
    shifts = lax.iota(jnp.int32, lag_pad) - (lag_count - 1) // 2
    angle_ids = jnp.mod(freqs[:, None] * shifts[None, :], 2 * total_bins)
    theta = angle_ids.astype(jnp.float32) * jnp.float32(math.pi / total_bins)
    return jnp.cos(theta), jnp.sin(theta)


LOW = 64
FBLOCK = 1024


def table_kernel(real_ref, imag_ref, chi_ref, shi_ref, clo_ref, slo_ref, out_ref, ctab, stab):
    @pl.when(pl.program_id(0) == 0)
    def _():
        out_ref[...] = jnp.zeros_like(out_ref)

    def fill(j, carry):
        clo = clo_ref[...]
        slo = slo_ref[...]
        ch = chi_ref[pl.ds(j, 1), :]
        sh = shi_ref[pl.ds(j, 1), :]
        rows = pl.ds(pl.multiple_of(j * LOW, LOW), LOW)
        ctab[rows, :] = (ch * clo - sh * slo).astype(jnp.bfloat16)
        stab[rows, :] = (-(sh * clo + ch * slo)).astype(jnp.bfloat16)
        return carry

    lax.fori_loop(0, FBLOCK // LOW, fill, 0)
    out_ref[...] += jnp.dot(real_ref[...], ctab[...], preferred_element_type=jnp.float32) + jnp.dot(
        imag_ref[...], stab[...], preferred_element_type=jnp.float32
    )


def correlate(real_all, imag_all, lag_count, total_bins):
    pair_count = real_all.shape[0]
    lag_pad = -(-lag_count // 128) * 128
    cos_hi, sin_hi = angle_table(lax.iota(jnp.int32, total_bins // LOW) * LOW, lag_pad, lag_count, total_bins)
    cos_lo, sin_lo = angle_table(lax.iota(jnp.int32, LOW), lag_pad, lag_count, total_bins)
    hi_rows = FBLOCK // LOW
    assert total_bins % FBLOCK == 0
    out = pl.pallas_call(
        table_kernel,
        grid=(total_bins // FBLOCK,),
        in_specs=[
            pl.BlockSpec((pair_count, FBLOCK), lambda i: (0, i)),
            pl.BlockSpec((pair_count, FBLOCK), lambda i: (0, i)),
            pl.BlockSpec((hi_rows, lag_pad), lambda i: (i, 0)),
            pl.BlockSpec((hi_rows, lag_pad), lambda i: (i, 0)),
            pl.BlockSpec((LOW, lag_pad), lambda i: (0, 0)),
            pl.BlockSpec((LOW, lag_pad), lambda i: (0, 0)),
        ],
        out_specs=pl.BlockSpec((pair_count, lag_pad), lambda i: (0, 0)),
        out_shape=jax.ShapeDtypeStruct((pair_count, lag_pad), jnp.float32),
        scratch_shapes=[
            pltpu.VMEM((FBLOCK, lag_pad), jnp.bfloat16),
            pltpu.VMEM((FBLOCK, lag_pad), jnp.bfloat16),
        ],
        compiler_params=pltpu.CompilerParams(
            dimension_semantics=("arbitrary",), vmem_limit_bytes=48 * 1024 * 1024
        ),
    )(real_all, imag_all, cos_hi, sin_hi, cos_lo, sin_lo)
    return out[:, :lag_count]


def local(spectra, stacks, pair_sta, pair_valid, owner, slot):
    total_bins = spectra.shape[2]
    lag_count = stacks.shape[1]
    stack_rows = stacks.shape[0]
    pair_count = pair_sta.shape[1]
    groups = lax.axis_size("grp")
    members = lax.axis_size("sta")
    devices = groups * members
    capacity = max(2, (4 * pair_count + 3 * devices - 1) // (3 * devices))
    whitened = whiten(spectra)
    gathered = lax.all_gather(whitened, "sta", axis=0, tiled=True)
    group_sta = gathered.shape[0]
    flat = gathered.reshape(group_sta, 2 * total_bins)
    sta_ids = lax.iota(jnp.int32, group_sta)[None, :]
    pick0 = (pair_sta[0][:, None] == sta_ids).astype(jnp.bfloat16)
    pick1 = (pair_sta[1][:, None] == sta_ids).astype(jnp.bfloat16)
    first = jnp.dot(pick0, flat, preferred_element_type=jnp.bfloat16).reshape(pair_count, 2, total_bins)
    second = jnp.dot(pick1, flat, preferred_element_type=jnp.bfloat16).reshape(pair_count, 2, total_bins)
    first = first.astype(jnp.float32)
    second = second.astype(jnp.float32)
    real_all = (first[:, 0] * second[:, 0] + first[:, 1] * second[:, 1]).astype(jnp.bfloat16)
    imag_all = (first[:, 1] * second[:, 0] - first[:, 0] * second[:, 1]).astype(jnp.bfloat16)

    corr = correlate(real_all, imag_all, lag_count, total_bins)
    corr = corr * jnp.float32(total_bins ** (-0.5)) * pair_valid.astype(jnp.float32)[:, None]
    dest = owner[:, 0]
    dest_hot = (dest[:, None] == lax.iota(jnp.int32, devices)[None, :]).astype(jnp.int32)
    before = jnp.cumsum(dest_hot, axis=0) - dest_hot
    position = jnp.sum(before * dest_hot, axis=1)
    flat = dest * capacity + position
    placing = (flat[:, None] == lax.iota(jnp.int32, devices * capacity)[None, :]).astype(
        jnp.float32
    )
    send_rows = jnp.dot(placing.T, corr, precision=lax.Precision.HIGHEST)
    send_slots = jnp.dot(
        placing.T, slot.astype(jnp.float32)[:, None], precision=lax.Precision.HIGHEST
    )[:, 0]
    got_rows, got_slots = (
        lax.all_to_all(
            send_rows.reshape(devices, capacity, lag_count),
            ("grp", "sta"),
            split_axis=0,
            concat_axis=0,
            tiled=True,
        ),
        lax.all_to_all(
            send_slots.reshape(devices, capacity),
            ("grp", "sta"),
            split_axis=0,
            concat_axis=0,
            tiled=True,
        ),
    )
    got_rows = got_rows.reshape(devices * capacity, lag_count)
    got_slots = got_slots.reshape(devices * capacity)
    adding = (
        got_slots[None, :] == lax.iota(jnp.int32, stack_rows).astype(jnp.float32)[:, None]
    ).astype(jnp.float32)
    return stacks + jnp.dot(adding, got_rows, precision=lax.Precision.HIGHEST)


def solution(mesh):
    return jax.shard_map(
        local,
        mesh=mesh,
        in_specs=(
            P(("grp", "sta"), None, None),
            P(("grp", "sta"), None),
            P(None, ("grp", "sta")),
            P(("grp", "sta")),
            P(("grp", "sta"), None),
            P(("grp", "sta")),
        ),
        out_specs=P(("grp", "sta"), None),
        check_vma=False,
    )
```

```python
import math

import jax
import jax.numpy as jnp
from jax import lax
from jax.experimental import pallas as pl
from jax.experimental.pallas import tpu as pltpu
from jax.sharding import PartitionSpec as P

BAND = 64


def whiten(spectra):
    shape = spectra.shape
    split = spectra.reshape(shape[0], 2, shape[2] // BAND, BAND)
    power = jnp.mean(split * split, axis=(1, 3), keepdims=True)
    return (split * lax.rsqrt(power + 1e-06)).reshape(shape).astype(jnp.bfloat16)


def angle_table(freqs, lag_pad, lag_count, total_bins):
    shifts = lax.iota(jnp.int32, lag_pad) - (lag_count - 1) // 2
    angle_ids = jnp.mod(freqs[:, None] * shifts[None, :], 2 * total_bins)
    theta = angle_ids.astype(jnp.float32) * jnp.float32(math.pi / total_bins)
    return jnp.cos(theta), jnp.sin(theta)


LOW = 64
FBLOCK = 1024


def table_kernel(a0_ref, a1_ref, b0_ref, b1_ref, chi_ref, shi_ref, clo_ref, slo_ref, out_ref, ctab, stab):
    @pl.when(pl.program_id(0) == 0)
    def _():
        out_ref[...] = jnp.zeros_like(out_ref)

    a0 = a0_ref[...].astype(jnp.float32)
    a1 = a1_ref[...].astype(jnp.float32)
    b0 = b0_ref[...].astype(jnp.float32)
    b1 = b1_ref[...].astype(jnp.float32)
    real = (a0 * b0 + a1 * b1).astype(jnp.bfloat16)
    imag = (a1 * b0 - a0 * b1).astype(jnp.bfloat16)

    def fill(j, carry):
        clo = clo_ref[...]
        slo = slo_ref[...]
        ch = chi_ref[pl.ds(j, 1), :]
        sh = shi_ref[pl.ds(j, 1), :]
        rows = pl.ds(pl.multiple_of(j * LOW, LOW), LOW)
        ctab[rows, :] = (ch * clo - sh * slo).astype(jnp.bfloat16)
        stab[rows, :] = (-(sh * clo + ch * slo)).astype(jnp.bfloat16)
        return carry

    lax.fori_loop(0, FBLOCK // LOW, fill, 0)
    out_ref[...] += jnp.dot(real, ctab[...], preferred_element_type=jnp.float32) + jnp.dot(
        imag, stab[...], preferred_element_type=jnp.float32
    )


def correlate(first, second, lag_count, total_bins):
    pair_count = first.shape[0]
    lag_pad = -(-(lag_count + 1) // 128) * 128
    cos_hi, sin_hi = angle_table(lax.iota(jnp.int32, total_bins // LOW) * LOW, lag_pad, lag_count, total_bins)
    cos_lo, sin_lo = angle_table(lax.iota(jnp.int32, LOW), lag_pad, lag_count, total_bins)
    hi_rows = FBLOCK // LOW
    assert total_bins % FBLOCK == 0
    blocks = total_bins // FBLOCK
    out = pl.pallas_call(
        table_kernel,
        grid=(total_bins // FBLOCK,),
        in_specs=[
            pl.BlockSpec((pair_count, FBLOCK), lambda i: (0, i)),
            pl.BlockSpec((pair_count, FBLOCK), lambda i: (0, i + blocks)),
            pl.BlockSpec((pair_count, FBLOCK), lambda i: (0, i)),
            pl.BlockSpec((pair_count, FBLOCK), lambda i: (0, i + blocks)),
            pl.BlockSpec((hi_rows, lag_pad), lambda i: (i, 0)),
            pl.BlockSpec((hi_rows, lag_pad), lambda i: (i, 0)),
            pl.BlockSpec((LOW, lag_pad), lambda i: (0, 0)),
            pl.BlockSpec((LOW, lag_pad), lambda i: (0, 0)),
        ],
        out_specs=pl.BlockSpec((pair_count, lag_pad), lambda i: (0, 0)),
        out_shape=jax.ShapeDtypeStruct((pair_count, lag_pad), jnp.float32),
        scratch_shapes=[
            pltpu.VMEM((FBLOCK, lag_pad), jnp.bfloat16),
            pltpu.VMEM((FBLOCK, lag_pad), jnp.bfloat16),
        ],
        compiler_params=pltpu.CompilerParams(
            dimension_semantics=("arbitrary",), vmem_limit_bytes=48 * 1024 * 1024
        ),
    )(first, first, second, second, cos_hi, sin_hi, cos_lo, sin_lo)
    return out


def local(spectra, stacks, pair_sta, pair_valid, owner, slot):
    total_bins = spectra.shape[2]
    lag_count = stacks.shape[1]
    stack_rows = stacks.shape[0]
    pair_count = pair_sta.shape[1]
    groups = lax.axis_size("grp")
    members = lax.axis_size("sta")
    devices = groups * members
    capacity = max(2, (4 * pair_count + 3 * devices - 1) // (3 * devices))
    whitened = whiten(spectra)
    gathered = lax.all_gather(whitened, "sta", axis=0, tiled=True)
    group_sta = gathered.shape[0]
    flat = gathered.reshape(group_sta, 2 * total_bins)
    sta_ids = lax.iota(jnp.int32, group_sta)[None, :]
    pick0 = (pair_sta[0][:, None] == sta_ids).astype(jnp.bfloat16)
    pick1 = (pair_sta[1][:, None] == sta_ids).astype(jnp.bfloat16)
    first = jnp.dot(pick0, flat, preferred_element_type=jnp.bfloat16)
    second = jnp.dot(pick1, flat, preferred_element_type=jnp.bfloat16)

    corr = correlate(first, second, lag_count, total_bins)
    corr = corr * jnp.float32(total_bins ** (-0.5)) * pair_valid.astype(jnp.float32)[:, None]
    column = lax.iota(jnp.int32, corr.shape[1])[None, :]
    corr = jnp.where(column == lag_count, slot.astype(jnp.float32)[:, None], corr)
    dest = owner[:, 0]
    dest_hot = (dest[:, None] == lax.iota(jnp.int32, devices)[None, :]).astype(jnp.int32)
    before = jnp.cumsum(dest_hot, axis=0) - dest_hot
    position = jnp.sum(before * dest_hot, axis=1)
    flat = dest * capacity + position
    placing = (flat[:, None] == lax.iota(jnp.int32, devices * capacity)[None, :]).astype(
        jnp.float32
    )
    send_rows = jnp.dot(placing.T, corr, precision=lax.Precision.HIGHEST)
    got = lax.all_to_all(
        send_rows.reshape(devices, capacity, corr.shape[1]),
        ("grp", "sta"),
        split_axis=0,
        concat_axis=0,
        tiled=True,
    ).reshape(devices * capacity, corr.shape[1])
    got_rows = got[:, :lag_count]
    got_slots = got[:, lag_count]
    adding = (
        got_slots[None, :] == lax.iota(jnp.int32, stack_rows).astype(jnp.float32)[:, None]
    ).astype(jnp.float32)
    return stacks + jnp.dot(adding, got_rows, precision=lax.Precision.HIGHEST)


def solution(mesh):
    return jax.shard_map(
        local,
        mesh=mesh,
        in_specs=(
            P(("grp", "sta"), None, None),
            P(("grp", "sta"), None),
            P(None, ("grp", "sta")),
            P(("grp", "sta")),
            P(("grp", "sta"), None),
            P(("grp", "sta")),
        ),
        out_specs=P(("grp", "sta"), None),
        check_vma=False,
    )
```

```python
import math

import jax
import jax.numpy as jnp
from jax import lax
from jax.experimental import pallas as pl
from jax.experimental.pallas import tpu as pltpu
from jax.sharding import PartitionSpec as P

BAND = 64


def whiten(spectra):
    shape = spectra.shape
    split = spectra.reshape(shape[0], 2, shape[2] // BAND, BAND)
    power = jnp.mean(split * split, axis=(1, 3), keepdims=True)
    return (split * lax.rsqrt(power + 1e-06)).reshape(shape).astype(jnp.bfloat16)


def angle_table(freqs, lag_pad, lag_count, total_bins):
    shifts = lax.iota(jnp.int32, lag_pad) - (lag_count - 1) // 2
    angle_ids = jnp.mod(freqs[:, None] * shifts[None, :], 2 * total_bins)
    theta = angle_ids.astype(jnp.float32) * jnp.float32(math.pi / total_bins)
    return jnp.cos(theta), jnp.sin(theta)


LOW = 64
FBLOCK = 1024
CHUNKS = 3


def table_kernel(a0_ref, a1_ref, b0_ref, b1_ref, chi_ref, shi_ref, clo_ref, slo_ref, acc_ref, out_ref, ctab, stab):
    @pl.when(pl.program_id(0) == 0)
    def _():
        out_ref[...] = acc_ref[...]

    a0 = a0_ref[...].astype(jnp.float32)
    a1 = a1_ref[...].astype(jnp.float32)
    b0 = b0_ref[...].astype(jnp.float32)
    b1 = b1_ref[...].astype(jnp.float32)
    real = (a0 * b0 + a1 * b1).astype(jnp.bfloat16)
    imag = (a1 * b0 - a0 * b1).astype(jnp.bfloat16)

    def fill(j, carry):
        clo = clo_ref[...]
        slo = slo_ref[...]
        ch = chi_ref[pl.ds(j, 1), :]
        sh = shi_ref[pl.ds(j, 1), :]
        rows = pl.ds(pl.multiple_of(j * LOW, LOW), LOW)
        ctab[rows, :] = (ch * clo - sh * slo).astype(jnp.bfloat16)
        stab[rows, :] = (-(sh * clo + ch * slo)).astype(jnp.bfloat16)
        return carry

    lax.fori_loop(0, FBLOCK // LOW, fill, 0)
    out_ref[...] += jnp.dot(real, ctab[...], preferred_element_type=jnp.float32) + jnp.dot(
        imag, stab[...], preferred_element_type=jnp.float32
    )


def correlate(first, second, tables, acc):
    cos_hi, sin_hi, cos_lo, sin_lo = tables
    pair_count = first.shape[0]
    lag_pad = cos_lo.shape[1]
    width = first.shape[1] // 2
    hi_rows = FBLOCK // LOW
    assert width % FBLOCK == 0
    blocks = width // FBLOCK
    out = pl.pallas_call(
        table_kernel,
        grid=(blocks,),
        in_specs=[
            pl.BlockSpec((pair_count, FBLOCK), lambda i: (0, i)),
            pl.BlockSpec((pair_count, FBLOCK), lambda i: (0, i + blocks)),
            pl.BlockSpec((pair_count, FBLOCK), lambda i: (0, i)),
            pl.BlockSpec((pair_count, FBLOCK), lambda i: (0, i + blocks)),
            pl.BlockSpec((hi_rows, lag_pad), lambda i: (i, 0)),
            pl.BlockSpec((hi_rows, lag_pad), lambda i: (i, 0)),
            pl.BlockSpec((LOW, lag_pad), lambda i: (0, 0)),
            pl.BlockSpec((LOW, lag_pad), lambda i: (0, 0)),
            pl.BlockSpec((pair_count, lag_pad), lambda i: (0, 0)),
        ],
        out_specs=pl.BlockSpec((pair_count, lag_pad), lambda i: (0, 0)),
        out_shape=jax.ShapeDtypeStruct((pair_count, lag_pad), jnp.float32),
        scratch_shapes=[
            pltpu.VMEM((FBLOCK, lag_pad), jnp.bfloat16),
            pltpu.VMEM((FBLOCK, lag_pad), jnp.bfloat16),
        ],
        compiler_params=pltpu.CompilerParams(
            dimension_semantics=("arbitrary",), vmem_limit_bytes=48 * 1024 * 1024
        ),
        cost_estimate=pl.CostEstimate(
            flops=2 * 2 * pair_count * width * lag_pad + 10 * width * lag_pad,
            transcendentals=0,
            bytes_accessed=4 * pair_count * width * 2 + 4 * pair_count * lag_pad,
        ),
        input_output_aliases={8: 0},
    )(first, first, second, second, cos_hi, sin_hi, cos_lo, sin_lo, acc)
    return out


def local(spectra, stacks, pair_sta, pair_valid, owner, slot):
    total_bins = spectra.shape[2]
    lag_count = stacks.shape[1]
    stack_rows = stacks.shape[0]
    pair_count = pair_sta.shape[1]
    groups = lax.axis_size("grp")
    members = lax.axis_size("sta")
    devices = groups * members
    capacity = max(2, (4 * pair_count + 3 * devices - 1) // (3 * devices))
    group_sta = spectra.shape[0] * members
    sta_ids = lax.iota(jnp.int32, group_sta)[None, :]
    pick0 = (pair_sta[0][:, None] == sta_ids).astype(jnp.bfloat16)
    pick1 = (pair_sta[1][:, None] == sta_ids).astype(jnp.bfloat16)
    lag_pad = -(-(lag_count + 1) // 128) * 128
    hi_all = angle_table(lax.iota(jnp.int32, total_bins // LOW) * LOW, lag_pad, lag_count, total_bins)
    lo_all = angle_table(lax.iota(jnp.int32, LOW), lag_pad, lag_count, total_bins)
    chunks = CHUNKS if total_bins % (CHUNKS * FBLOCK) == 0 else 1
    width = total_bins // chunks
    corr = jnp.zeros((pair_count, lag_pad), jnp.float32)
    for c in range(chunks):
        piece = whiten(spectra[:, :, c * width:(c + 1) * width])
        gathered = lax.all_gather(piece, "sta", axis=0, tiled=True)
        if c:
            gathered, corr = lax.optimization_barrier((gathered, corr))
        flat = gathered.reshape(group_sta, 2 * width)
        first = jnp.dot(pick0, flat, preferred_element_type=jnp.bfloat16)
        second = jnp.dot(pick1, flat, preferred_element_type=jnp.bfloat16)
        rows = slice(c * width // LOW, (c + 1) * width // LOW)
        tables = (hi_all[0][rows], hi_all[1][rows], lo_all[0], lo_all[1])
        corr = correlate(first, second, tables, corr)
    corr = corr * jnp.float32(total_bins ** (-0.5)) * pair_valid.astype(jnp.float32)[:, None]
    column = lax.iota(jnp.int32, corr.shape[1])[None, :]
    corr = jnp.where(column == lag_count, slot.astype(jnp.float32)[:, None], corr)
    dest = owner[:, 0]
    dest_hot = (dest[:, None] == lax.iota(jnp.int32, devices)[None, :]).astype(jnp.int32)
    before = jnp.cumsum(dest_hot, axis=0) - dest_hot
    position = jnp.sum(before * dest_hot, axis=1)
    flat = dest * capacity + position
    placing = (flat[:, None] == lax.iota(jnp.int32, devices * capacity)[None, :]).astype(
        jnp.float32
    )
    send_rows = jnp.dot(placing.T, corr, precision=lax.Precision.HIGHEST)
    got = lax.all_to_all(
        send_rows.reshape(devices, capacity, corr.shape[1]),
        ("grp", "sta"),
        split_axis=0,
        concat_axis=0,
        tiled=True,
    ).reshape(devices * capacity, corr.shape[1])
    got_rows = got[:, :lag_count]
    got_slots = got[:, lag_count]
    adding = (
        got_slots[None, :] == lax.iota(jnp.int32, stack_rows).astype(jnp.float32)[:, None]
    ).astype(jnp.float32)
    return stacks + jnp.dot(adding, got_rows, precision=lax.Precision.HIGHEST)


def solution(mesh):
    return jax.shard_map(
        local,
        mesh=mesh,
        in_specs=(
            P(("grp", "sta"), None, None),
            P(("grp", "sta"), None),
            P(None, ("grp", "sta")),
            P(("grp", "sta")),
            P(("grp", "sta"), None),
            P(("grp", "sta")),
        ),
        out_specs=P(("grp", "sta"), None),
        check_vma=False,
    )
```

```python
import math

import jax
import jax.numpy as jnp
from jax import lax
from jax.experimental import pallas as pl
from jax.experimental.pallas import tpu as pltpu
from jax.sharding import PartitionSpec as P

BAND = 64


def whiten(spectra):
    shape = spectra.shape
    split = spectra.reshape(shape[0], 2, shape[2] // BAND, BAND)
    power = jnp.mean(split * split, axis=(1, 3), keepdims=True)
    return (split * lax.rsqrt(power + 1e-06)).reshape(shape).astype(jnp.bfloat16)


def angle_table(freqs, lag_pad, total_bins):
    shifts = lax.iota(jnp.int32, lag_pad)
    angle_ids = jnp.mod(freqs[:, None] * shifts[None, :], 2 * total_bins)
    theta = angle_ids.astype(jnp.float32) * jnp.float32(math.pi / total_bins)
    return jnp.cos(theta), jnp.sin(theta)


LOW = 64
FBLOCK = 1024
CHUNKS = 3


def table_kernel(a0_ref, a1_ref, b0_ref, b1_ref, chi_ref, shi_ref, clo_ref, slo_ref, acc_ref, out_ref, ctab, stab):
    @pl.when(pl.program_id(0) == 0)
    def _():
        out_ref[...] = acc_ref[...]

    a0 = a0_ref[...].astype(jnp.float32)
    a1 = a1_ref[...].astype(jnp.float32)
    b0 = b0_ref[...].astype(jnp.float32)
    b1 = b1_ref[...].astype(jnp.float32)
    real = (a0 * b0 + a1 * b1).astype(jnp.bfloat16)
    imag = (a1 * b0 - a0 * b1).astype(jnp.bfloat16)

    def fill(j, carry):
        clo = clo_ref[...]
        slo = slo_ref[...]
        ch = chi_ref[pl.ds(j, 1), :]
        sh = shi_ref[pl.ds(j, 1), :]
        rows = pl.ds(pl.multiple_of(j * LOW, LOW), LOW)
        ctab[rows, :] = (ch * clo - sh * slo).astype(jnp.bfloat16)
        stab[rows, :] = (sh * clo + ch * slo).astype(jnp.bfloat16)
        return carry

    lax.fori_loop(0, FBLOCK // LOW, fill, 0)
    half = ctab.shape[1]
    out_ref[:, :half] += jnp.dot(real, ctab[...], preferred_element_type=jnp.float32)
    out_ref[:, half:] += jnp.dot(imag, stab[...], preferred_element_type=jnp.float32)


def correlate(first, second, tables, acc):
    cos_hi, sin_hi, cos_lo, sin_lo = tables
    pair_count = first.shape[0]
    lag_pad = cos_lo.shape[1]
    width = first.shape[1] // 2
    hi_rows = FBLOCK // LOW
    assert width % FBLOCK == 0
    blocks = width // FBLOCK
    out = pl.pallas_call(
        table_kernel,
        grid=(blocks,),
        in_specs=[
            pl.BlockSpec((pair_count, FBLOCK), lambda i: (0, i)),
            pl.BlockSpec((pair_count, FBLOCK), lambda i: (0, i + blocks)),
            pl.BlockSpec((pair_count, FBLOCK), lambda i: (0, i)),
            pl.BlockSpec((pair_count, FBLOCK), lambda i: (0, i + blocks)),
            pl.BlockSpec((hi_rows, lag_pad), lambda i: (i, 0)),
            pl.BlockSpec((hi_rows, lag_pad), lambda i: (i, 0)),
            pl.BlockSpec((LOW, lag_pad), lambda i: (0, 0)),
            pl.BlockSpec((LOW, lag_pad), lambda i: (0, 0)),
            pl.BlockSpec((pair_count, 2 * lag_pad), lambda i: (0, 0)),
        ],
        out_specs=pl.BlockSpec((pair_count, 2 * lag_pad), lambda i: (0, 0)),
        out_shape=jax.ShapeDtypeStruct((pair_count, 2 * lag_pad), jnp.float32),
        scratch_shapes=[
            pltpu.VMEM((FBLOCK, lag_pad), jnp.bfloat16),
            pltpu.VMEM((FBLOCK, lag_pad), jnp.bfloat16),
        ],
        compiler_params=pltpu.CompilerParams(
            dimension_semantics=("arbitrary",), vmem_limit_bytes=48 * 1024 * 1024
        ),
        cost_estimate=pl.CostEstimate(
            flops=2 * 2 * pair_count * width * lag_pad + 10 * width * lag_pad,
            transcendentals=0,
            bytes_accessed=4 * pair_count * width * 2 + 4 * pair_count * lag_pad,
        ),
        input_output_aliases={8: 0},
    )(first, first, second, second, cos_hi, sin_hi, cos_lo, sin_lo, acc)
    return out


def local(spectra, stacks, pair_sta, pair_valid, owner, slot):
    total_bins = spectra.shape[2]
    lag_count = stacks.shape[1]
    stack_rows = stacks.shape[0]
    pair_count = pair_sta.shape[1]
    groups = lax.axis_size("grp")
    members = lax.axis_size("sta")
    devices = groups * members
    capacity = max(2, (4 * pair_count + 3 * devices - 1) // (3 * devices))
    group_sta = spectra.shape[0] * members
    sta_ids = lax.iota(jnp.int32, group_sta)[None, :]
    pick0 = (pair_sta[0][:, None] == sta_ids).astype(jnp.bfloat16)
    pick1 = (pair_sta[1][:, None] == sta_ids).astype(jnp.bfloat16)
    assert lag_count % 2 == 1
    side = (lag_count - 1) // 2
    lag_pad = -(-(side + 1) // 128) * 128
    hi_all = angle_table(lax.iota(jnp.int32, total_bins // LOW) * LOW, lag_pad, total_bins)
    lo_all = angle_table(lax.iota(jnp.int32, LOW), lag_pad, total_bins)
    chunks = CHUNKS if total_bins % (CHUNKS * FBLOCK) == 0 else 1
    width = total_bins // chunks
    corr = jnp.zeros((pair_count, 2 * lag_pad), jnp.float32)
    for c in range(chunks):
        piece = whiten(spectra[:, :, c * width:(c + 1) * width])
        gathered = lax.all_gather(piece, "sta", axis=0, tiled=True)
        if c:
            gathered, corr = lax.optimization_barrier((gathered, corr))
        flat = gathered.reshape(group_sta, 2 * width)
        first = jnp.dot(pick0, flat, preferred_element_type=jnp.bfloat16)
        second = jnp.dot(pick1, flat, preferred_element_type=jnp.bfloat16)
        rows = slice(c * width // LOW, (c + 1) * width // LOW)
        tables = (hi_all[0][rows], hi_all[1][rows], lo_all[0], lo_all[1])
        corr = correlate(first, second, tables, corr)
    even = corr[:, : side + 1]
    odd = corr[:, lag_pad : lag_pad + side + 1]
    corr = jnp.concatenate([(even + odd)[:, :0:-1], even - odd], axis=1)
    corr = corr * jnp.float32(total_bins ** (-0.5)) * pair_valid.astype(jnp.float32)[:, None]
    lag_ext = -(-(lag_count + 1) // 128) * 128
    corr = jnp.concatenate(
        [corr, slot.astype(jnp.float32)[:, None], jnp.zeros((pair_count, lag_ext - lag_count - 1), jnp.float32)],
        axis=1,
    )
    dest = owner[:, 0]
    dest_hot = (dest[:, None] == lax.iota(jnp.int32, devices)[None, :]).astype(jnp.int32)
    before = jnp.cumsum(dest_hot, axis=0) - dest_hot
    position = jnp.sum(before * dest_hot, axis=1)
    flat = dest * capacity + position
    placing = (flat[:, None] == lax.iota(jnp.int32, devices * capacity)[None, :]).astype(
        jnp.float32
    )
    send_rows = jnp.dot(placing.T, corr, precision=lax.Precision.HIGHEST)
    got = lax.all_to_all(
        send_rows.reshape(devices, capacity, corr.shape[1]),
        ("grp", "sta"),
        split_axis=0,
        concat_axis=0,
        tiled=True,
    ).reshape(devices * capacity, corr.shape[1])
    got_rows = got[:, :lag_count]
    got_slots = got[:, lag_count]
    adding = (
        got_slots[None, :] == lax.iota(jnp.int32, stack_rows).astype(jnp.float32)[:, None]
    ).astype(jnp.float32)
    return stacks + jnp.dot(adding, got_rows, precision=lax.Precision.HIGHEST)


def solution(mesh):
    return jax.shard_map(
        local,
        mesh=mesh,
        in_specs=(
            P(("grp", "sta"), None, None),
            P(("grp", "sta"), None),
            P(None, ("grp", "sta")),
            P(("grp", "sta")),
            P(("grp", "sta"), None),
            P(("grp", "sta")),
        ),
        out_specs=P(("grp", "sta"), None),
        check_vma=False,
    )
```

```python
import math

import jax
import jax.numpy as jnp
from jax import lax
from jax.experimental import pallas as pl
from jax.experimental.pallas import tpu as pltpu
from jax.sharding import PartitionSpec as P

BAND = 64


def whiten(spectra):
    shape = spectra.shape
    split = spectra.reshape(shape[0], 2, shape[2] // BAND, BAND)
    power = jnp.mean(split * split, axis=(1, 3), keepdims=True)
    return (split * lax.rsqrt(power + 1e-06)).reshape(shape).astype(jnp.bfloat16)


def angle_table(freqs, lag_pad, total_bins):
    shifts = lax.iota(jnp.int32, lag_pad)
    angle_ids = jnp.mod(freqs[:, None] * shifts[None, :], 2 * total_bins)
    theta = angle_ids.astype(jnp.float32) * jnp.float32(math.pi / total_bins)
    return jnp.cos(theta), jnp.sin(theta)


LOW = 64
FBLOCK = 1024


def table_kernel(a0_ref, a1_ref, b0_ref, b1_ref, chi_ref, shi_ref, clo_ref, slo_ref, acc_ref, out_ref, ctab, stab):
    @pl.when(pl.program_id(0) == 0)
    def _():
        out_ref[...] = acc_ref[...]

    a0 = a0_ref[...].astype(jnp.float32)
    a1 = a1_ref[...].astype(jnp.float32)
    b0 = b0_ref[...].astype(jnp.float32)
    b1 = b1_ref[...].astype(jnp.float32)
    real = (a0 * b0 + a1 * b1).astype(jnp.bfloat16)
    imag = (a1 * b0 - a0 * b1).astype(jnp.bfloat16)

    def fill(j, carry):
        clo = clo_ref[...]
        slo = slo_ref[...]
        ch = chi_ref[pl.ds(j, 1), :]
        sh = shi_ref[pl.ds(j, 1), :]
        rows = pl.ds(pl.multiple_of(j * LOW, LOW), LOW)
        ctab[rows, :] = (ch * clo - sh * slo).astype(jnp.bfloat16)
        stab[rows, :] = (sh * clo + ch * slo).astype(jnp.bfloat16)
        return carry

    lax.fori_loop(0, FBLOCK // LOW, fill, 0)
    half = ctab.shape[1]
    out_ref[:, :half] += jnp.dot(real, ctab[...], preferred_element_type=jnp.float32)
    out_ref[:, half:] += jnp.dot(imag, stab[...], preferred_element_type=jnp.float32)


def correlate(first, second, tables, acc):
    cos_hi, sin_hi, cos_lo, sin_lo = tables
    pair_count = first.shape[0]
    lag_pad = cos_lo.shape[1]
    width = first.shape[1] // 2
    hi_rows = FBLOCK // LOW
    assert width % FBLOCK == 0
    blocks = width // FBLOCK
    out = pl.pallas_call(
        table_kernel,
        grid=(blocks,),
        in_specs=[
            pl.BlockSpec((pair_count, FBLOCK), lambda i: (0, i)),
            pl.BlockSpec((pair_count, FBLOCK), lambda i: (0, i + blocks)),
            pl.BlockSpec((pair_count, FBLOCK), lambda i: (0, i)),
            pl.BlockSpec((pair_count, FBLOCK), lambda i: (0, i + blocks)),
            pl.BlockSpec((hi_rows, lag_pad), lambda i: (i, 0)),
            pl.BlockSpec((hi_rows, lag_pad), lambda i: (i, 0)),
            pl.BlockSpec((LOW, lag_pad), lambda i: (0, 0)),
            pl.BlockSpec((LOW, lag_pad), lambda i: (0, 0)),
            pl.BlockSpec((pair_count, 2 * lag_pad), lambda i: (0, 0)),
        ],
        out_specs=pl.BlockSpec((pair_count, 2 * lag_pad), lambda i: (0, 0)),
        out_shape=jax.ShapeDtypeStruct((pair_count, 2 * lag_pad), jnp.float32),
        scratch_shapes=[
            pltpu.VMEM((FBLOCK, lag_pad), jnp.bfloat16),
            pltpu.VMEM((FBLOCK, lag_pad), jnp.bfloat16),
        ],
        compiler_params=pltpu.CompilerParams(
            dimension_semantics=("arbitrary",), vmem_limit_bytes=48 * 1024 * 1024
        ),
        cost_estimate=pl.CostEstimate(
            flops=2 * 2 * pair_count * width * lag_pad + 10 * width * lag_pad,
            transcendentals=0,
            bytes_accessed=4 * pair_count * width * 2 + 4 * pair_count * lag_pad,
        ),
        input_output_aliases={8: 0},
    )(first, first, second, second, cos_hi, sin_hi, cos_lo, sin_lo, acc)
    return out


def local(spectra, stacks, pair_sta, pair_valid, owner, slot):
    total_bins = spectra.shape[2]
    lag_count = stacks.shape[1]
    stack_rows = stacks.shape[0]
    pair_count = pair_sta.shape[1]
    groups = lax.axis_size("grp")
    members = lax.axis_size("sta")
    devices = groups * members
    capacity = max(2, (4 * pair_count + 3 * devices - 1) // (3 * devices))
    group_sta = spectra.shape[0] * members
    sta_ids = lax.iota(jnp.int32, group_sta)[None, :]
    pick0 = (pair_sta[0][:, None] == sta_ids).astype(jnp.bfloat16)
    pick1 = (pair_sta[1][:, None] == sta_ids).astype(jnp.bfloat16)
    assert lag_count % 2 == 1
    side = (lag_count - 1) // 2
    lag_pad = -(-(side + 1) // 128) * 128
    hi_all = angle_table(lax.iota(jnp.int32, total_bins // LOW) * LOW, lag_pad, total_bins)
    lo_all = angle_table(lax.iota(jnp.int32, LOW), lag_pad, total_bins)
    blocks = total_bins // FBLOCK
    assert total_bins % FBLOCK == 0
    lead = max(1, min(blocks - 1, (blocks * 31 + 25) // 50))
    bounds = [0, lead * FBLOCK, total_bins] if blocks > 1 else [0, total_bins]
    corr = jnp.zeros((pair_count, 2 * lag_pad), jnp.float32)
    for c in range(len(bounds) - 1):
        begin, end = bounds[c], bounds[c + 1]
        width = end - begin
        piece = whiten(spectra[:, :, begin:end])
        gathered = lax.all_gather(piece, "sta", axis=0, tiled=True)
        if c:
            gathered, corr = lax.optimization_barrier((gathered, corr))
        flat = gathered.reshape(group_sta, 2 * width)
        first = jnp.dot(pick0, flat, preferred_element_type=jnp.bfloat16)
        second = jnp.dot(pick1, flat, preferred_element_type=jnp.bfloat16)
        rows = slice(begin // LOW, end // LOW)
        tables = (hi_all[0][rows], hi_all[1][rows], lo_all[0], lo_all[1])
        corr = correlate(first, second, tables, corr)
    even = corr[:, : side + 1]
    odd = corr[:, lag_pad : lag_pad + side + 1]
    corr = jnp.concatenate([(even + odd)[:, :0:-1], even - odd], axis=1)
    corr = corr * jnp.float32(total_bins ** (-0.5)) * pair_valid.astype(jnp.float32)[:, None]
    lag_ext = -(-(lag_count + 1) // 128) * 128
    corr = jnp.concatenate(
        [corr, slot.astype(jnp.float32)[:, None], jnp.zeros((pair_count, lag_ext - lag_count - 1), jnp.float32)],
        axis=1,
    )
    dest = owner[:, 0]
    dest_hot = (dest[:, None] == lax.iota(jnp.int32, devices)[None, :]).astype(jnp.int32)
    before = jnp.cumsum(dest_hot, axis=0) - dest_hot
    position = jnp.sum(before * dest_hot, axis=1)
    flat = dest * capacity + position
    placing = (flat[:, None] == lax.iota(jnp.int32, devices * capacity)[None, :]).astype(
        jnp.float32
    )
    send_rows = jnp.dot(placing.T, corr, precision=lax.Precision.HIGHEST)
    got = lax.all_to_all(
        send_rows.reshape(devices, capacity, corr.shape[1]),
        ("grp", "sta"),
        split_axis=0,
        concat_axis=0,
        tiled=True,
    ).reshape(devices * capacity, corr.shape[1])
    got_rows = got[:, :lag_count]
    got_slots = got[:, lag_count]
    adding = (
        got_slots[None, :] == lax.iota(jnp.int32, stack_rows).astype(jnp.float32)[:, None]
    ).astype(jnp.float32)
    return stacks + jnp.dot(adding, got_rows, precision=lax.Precision.HIGHEST)


def solution(mesh):
    return jax.shard_map(
        local,
        mesh=mesh,
        in_specs=(
            P(("grp", "sta"), None, None),
            P(("grp", "sta"), None),
            P(None, ("grp", "sta")),
            P(("grp", "sta")),
            P(("grp", "sta"), None),
            P(("grp", "sta")),
        ),
        out_specs=P(("grp", "sta"), None),
        check_vma=False,
    )
```

```python
import math

import jax
import jax.numpy as jnp
from jax import lax
from jax.experimental import pallas as pl
from jax.experimental.pallas import tpu as pltpu
from jax.sharding import PartitionSpec as P

BAND = 64


def whiten(spectra):
    shape = spectra.shape
    split = spectra.reshape(shape[0], 2, shape[2] // BAND, BAND)
    power = jnp.mean(split * split, axis=(1, 3), keepdims=True)
    return (split * lax.rsqrt(power + 1e-06)).reshape(shape).astype(jnp.bfloat16)


def angle_table(freqs, lag_pad, total_bins):
    shifts = lax.iota(jnp.int32, lag_pad)
    angle_ids = jnp.mod(freqs[:, None] * shifts[None, :], 2 * total_bins)
    theta = angle_ids.astype(jnp.float32) * jnp.float32(math.pi / total_bins)
    return jnp.cos(theta), jnp.sin(theta)


LOW = 64
FBLOCK = 1024


def table_kernel(a0_ref, a1_ref, b0_ref, b1_ref, chi_ref, shi_ref, clo_ref, slo_ref, acc_ref, out_ref, ctab, stab):
    @pl.when(pl.program_id(0) == 0)
    def _():
        out_ref[...] = acc_ref[...]

    a0 = a0_ref[...].astype(jnp.float32)
    a1 = a1_ref[...].astype(jnp.float32)
    b0 = b0_ref[...].astype(jnp.float32)
    b1 = b1_ref[...].astype(jnp.float32)
    real = (a0 * b0 + a1 * b1).astype(jnp.bfloat16)
    imag = (a1 * b0 - a0 * b1).astype(jnp.bfloat16)

    def fill(j, carry):
        clo = clo_ref[...]
        slo = slo_ref[...]
        ch = chi_ref[pl.ds(j, 1), :]
        sh = shi_ref[pl.ds(j, 1), :]
        rows = pl.ds(pl.multiple_of(j * LOW, LOW), LOW)
        ctab[rows, :] = (ch * clo - sh * slo).astype(jnp.bfloat16)
        stab[rows, :] = (sh * clo + ch * slo).astype(jnp.bfloat16)
        return carry

    lax.fori_loop(0, FBLOCK // LOW, fill, 0)
    half = ctab.shape[1]
    out_ref[:, :half] += jnp.dot(real, ctab[...], preferred_element_type=jnp.float32)
    out_ref[:, half:] += jnp.dot(imag, stab[...], preferred_element_type=jnp.float32)


def correlate(first, second, tables, acc):
    cos_hi, sin_hi, cos_lo, sin_lo = tables
    pair_count = first.shape[0]
    lag_pad = cos_lo.shape[1]
    width = first.shape[1] // 2
    hi_rows = FBLOCK // LOW
    assert width % FBLOCK == 0
    blocks = width // FBLOCK
    out = pl.pallas_call(
        table_kernel,
        grid=(blocks,),
        in_specs=[
            pl.BlockSpec((pair_count, FBLOCK), lambda i: (0, i)),
            pl.BlockSpec((pair_count, FBLOCK), lambda i: (0, i + blocks)),
            pl.BlockSpec((pair_count, FBLOCK), lambda i: (0, i)),
            pl.BlockSpec((pair_count, FBLOCK), lambda i: (0, i + blocks)),
            pl.BlockSpec((hi_rows, lag_pad), lambda i: (i, 0)),
            pl.BlockSpec((hi_rows, lag_pad), lambda i: (i, 0)),
            pl.BlockSpec((LOW, lag_pad), lambda i: (0, 0)),
            pl.BlockSpec((LOW, lag_pad), lambda i: (0, 0)),
            pl.BlockSpec((pair_count, 2 * lag_pad), lambda i: (0, 0)),
        ],
        out_specs=pl.BlockSpec((pair_count, 2 * lag_pad), lambda i: (0, 0)),
        out_shape=jax.ShapeDtypeStruct((pair_count, 2 * lag_pad), jnp.float32),
        scratch_shapes=[
            pltpu.VMEM((FBLOCK, lag_pad), jnp.bfloat16),
            pltpu.VMEM((FBLOCK, lag_pad), jnp.bfloat16),
        ],
        compiler_params=pltpu.CompilerParams(
            dimension_semantics=("arbitrary",), vmem_limit_bytes=48 * 1024 * 1024
        ),
        cost_estimate=pl.CostEstimate(
            flops=2 * 2 * pair_count * width * lag_pad + 10 * width * lag_pad,
            transcendentals=0,
            bytes_accessed=4 * pair_count * width * 2 + 4 * pair_count * lag_pad,
        ),
        input_output_aliases={8: 0},
    )(first, first, second, second, cos_hi, sin_hi, cos_lo, sin_lo, acc)
    return out


def local(spectra, stacks, pair_sta, pair_valid, owner, slot):
    total_bins = spectra.shape[2]
    lag_count = stacks.shape[1]
    stack_rows = stacks.shape[0]
    pair_count = pair_sta.shape[1]
    groups = lax.axis_size("grp")
    members = lax.axis_size("sta")
    devices = groups * members
    capacity = max(2, (4 * pair_count + 3 * devices - 1) // (3 * devices))
    per = spectra.shape[0]
    group_sta = per * members
    me = lax.axis_index("sta")
    source = jnp.mod(me - lax.iota(jnp.int32, members), members)
    sta_ids = (source[:, None] * per + lax.iota(jnp.int32, per)[None, :]).reshape(1, group_sta)
    pick0 = (pair_sta[0][:, None] == sta_ids).astype(jnp.bfloat16)
    pick1 = (pair_sta[1][:, None] == sta_ids).astype(jnp.bfloat16)
    assert lag_count % 2 == 1
    side = (lag_count - 1) // 2
    lag_pad = -(-(side + 1) // 128) * 128
    hi_all = angle_table(lax.iota(jnp.int32, total_bins // LOW) * LOW, lag_pad, total_bins)
    lo_all = angle_table(lax.iota(jnp.int32, LOW), lag_pad, total_bins)
    blocks = total_bins // FBLOCK
    assert total_bins % FBLOCK == 0
    lead = max(1, min(blocks - 1, (blocks * 31 + 25) // 50))
    bounds = [0, lead * FBLOCK, total_bins] if blocks > 1 else [0, total_bins]
    corr = jnp.zeros((pair_count, 2 * lag_pad), jnp.float32)
    for c in range(len(bounds) - 1):
        begin, end = bounds[c], bounds[c + 1]
        width = end - begin
        piece = whiten(spectra[:, :, begin:end])
        parts = [piece]
        for k in range(1, members):
            shift = [(j, (j + k) % members) for j in range(members)]
            parts.append(lax.ppermute(piece, "sta", shift))
        gathered = jnp.concatenate(parts, axis=0)
        if c:
            gathered, corr = lax.optimization_barrier((gathered, corr))
        flat = gathered.reshape(group_sta, 2 * width)
        first = jnp.dot(pick0, flat, preferred_element_type=jnp.bfloat16)
        second = jnp.dot(pick1, flat, preferred_element_type=jnp.bfloat16)
        rows = slice(begin // LOW, end // LOW)
        tables = (hi_all[0][rows], hi_all[1][rows], lo_all[0], lo_all[1])
        corr = correlate(first, second, tables, corr)
    even = corr[:, : side + 1]
    odd = corr[:, lag_pad : lag_pad + side + 1]
    corr = jnp.concatenate([(even + odd)[:, :0:-1], even - odd], axis=1)
    corr = corr * jnp.float32(total_bins ** (-0.5)) * pair_valid.astype(jnp.float32)[:, None]
    lag_ext = -(-(lag_count + 1) // 128) * 128
    corr = jnp.concatenate(
        [corr, slot.astype(jnp.float32)[:, None], jnp.zeros((pair_count, lag_ext - lag_count - 1), jnp.float32)],
        axis=1,
    )
    dest = owner[:, 0]
    dest_hot = (dest[:, None] == lax.iota(jnp.int32, devices)[None, :]).astype(jnp.int32)
    before = jnp.cumsum(dest_hot, axis=0) - dest_hot
    position = jnp.sum(before * dest_hot, axis=1)
    flat = dest * capacity + position
    placing = (flat[:, None] == lax.iota(jnp.int32, devices * capacity)[None, :]).astype(
        jnp.float32
    )
    send_rows = jnp.dot(placing.T, corr, precision=lax.Precision.HIGHEST)
    got = lax.all_to_all(
        send_rows.reshape(devices, capacity, corr.shape[1]),
        ("grp", "sta"),
        split_axis=0,
        concat_axis=0,
        tiled=True,
    ).reshape(devices * capacity, corr.shape[1])
    got_rows = got[:, :lag_count]
    got_slots = got[:, lag_count]
    adding = (
        got_slots[None, :] == lax.iota(jnp.int32, stack_rows).astype(jnp.float32)[:, None]
    ).astype(jnp.float32)
    return stacks + jnp.dot(adding, got_rows, precision=lax.Precision.HIGHEST)


def solution(mesh):
    return jax.shard_map(
        local,
        mesh=mesh,
        in_specs=(
            P(("grp", "sta"), None, None),
            P(("grp", "sta"), None),
            P(None, ("grp", "sta")),
            P(("grp", "sta")),
            P(("grp", "sta"), None),
            P(("grp", "sta")),
        ),
        out_specs=P(("grp", "sta"), None),
        check_vma=False,
    )
```

```python
import math

import jax
import jax.numpy as jnp
from jax import lax
from jax.experimental import pallas as pl
from jax.experimental.pallas import tpu as pltpu
from jax.sharding import PartitionSpec as P

BAND = 64


def whiten(spectra):
    shape = spectra.shape
    split = spectra.reshape(shape[0], 2, shape[2] // BAND, BAND)
    power = jnp.mean(split * split, axis=(1, 3), keepdims=True)
    return (split * lax.rsqrt(power + 1e-06)).reshape(shape).astype(jnp.bfloat16)


def angle_table(freqs, lag_pad, total_bins):
    shifts = lax.iota(jnp.int32, lag_pad)
    angle_ids = jnp.mod(freqs[:, None] * shifts[None, :], 2 * total_bins)
    theta = angle_ids.astype(jnp.float32) * jnp.float32(math.pi / total_bins)
    return jnp.cos(theta), jnp.sin(theta)


LOW = 64
FBLOCK = 1024


def table_kernel(a0_ref, a1_ref, b0_ref, b1_ref, chi_ref, shi_ref, clo_ref, slo_ref, acc_ref, out_ref, ctab, stab):
    @pl.when(pl.program_id(0) == 0)
    def _():
        out_ref[...] = acc_ref[...]

    a0 = a0_ref[...].astype(jnp.float32)
    a1 = a1_ref[...].astype(jnp.float32)
    b0 = b0_ref[...].astype(jnp.float32)
    b1 = b1_ref[...].astype(jnp.float32)
    real = (a0 * b0 + a1 * b1).astype(jnp.bfloat16)
    imag = (a1 * b0 - a0 * b1).astype(jnp.bfloat16)

    def fill(j, carry):
        clo = clo_ref[...]
        slo = slo_ref[...]
        ch = chi_ref[pl.ds(j, 1), :]
        sh = shi_ref[pl.ds(j, 1), :]
        rows = pl.ds(pl.multiple_of(j * LOW, LOW), LOW)
        ctab[rows, :] = (ch * clo - sh * slo).astype(jnp.bfloat16)
        stab[rows, :] = (sh * clo + ch * slo).astype(jnp.bfloat16)
        return carry

    lax.fori_loop(0, FBLOCK // LOW, fill, 0)
    half = ctab.shape[1]
    out_ref[:, :half] += jnp.dot(real, ctab[...], preferred_element_type=jnp.float32)
    out_ref[:, half:] += jnp.dot(imag, stab[...], preferred_element_type=jnp.float32)


def correlate(both, tables, acc):
    cos_hi, sin_hi, cos_lo, sin_lo = tables
    pair_count = both.shape[0] // 2
    lag_pad = cos_lo.shape[1]
    width = both.shape[1] // 2
    hi_rows = FBLOCK // LOW
    assert width % FBLOCK == 0
    blocks = width // FBLOCK
    out = pl.pallas_call(
        table_kernel,
        grid=(blocks,),
        in_specs=[
            pl.BlockSpec((pair_count, FBLOCK), lambda i: (0, i)),
            pl.BlockSpec((pair_count, FBLOCK), lambda i: (0, i + blocks)),
            pl.BlockSpec((pair_count, FBLOCK), lambda i: (1, i)),
            pl.BlockSpec((pair_count, FBLOCK), lambda i: (1, i + blocks)),
            pl.BlockSpec((hi_rows, lag_pad), lambda i: (i, 0)),
            pl.BlockSpec((hi_rows, lag_pad), lambda i: (i, 0)),
            pl.BlockSpec((LOW, lag_pad), lambda i: (0, 0)),
            pl.BlockSpec((LOW, lag_pad), lambda i: (0, 0)),
            pl.BlockSpec((pair_count, 2 * lag_pad), lambda i: (0, 0)),
        ],
        out_specs=pl.BlockSpec((pair_count, 2 * lag_pad), lambda i: (0, 0)),
        out_shape=jax.ShapeDtypeStruct((pair_count, 2 * lag_pad), jnp.float32),
        scratch_shapes=[
            pltpu.VMEM((FBLOCK, lag_pad), jnp.bfloat16),
            pltpu.VMEM((FBLOCK, lag_pad), jnp.bfloat16),
        ],
        compiler_params=pltpu.CompilerParams(
            dimension_semantics=("arbitrary",), vmem_limit_bytes=48 * 1024 * 1024
        ),
        cost_estimate=pl.CostEstimate(
            flops=2 * 2 * pair_count * width * lag_pad + 10 * width * lag_pad,
            transcendentals=0,
            bytes_accessed=4 * pair_count * width * 2 + 4 * pair_count * lag_pad,
        ),
        input_output_aliases={8: 0},
    )(both, both, both, both, cos_hi, sin_hi, cos_lo, sin_lo, acc)
    return out


def local(spectra, stacks, pair_sta, pair_valid, owner, slot):
    total_bins = spectra.shape[2]
    lag_count = stacks.shape[1]
    stack_rows = stacks.shape[0]
    pair_count = pair_sta.shape[1]
    groups = lax.axis_size("grp")
    members = lax.axis_size("sta")
    devices = groups * members
    capacity = max(2, (4 * pair_count + 3 * devices - 1) // (3 * devices))
    group_sta = spectra.shape[0] * members
    sta_ids = lax.iota(jnp.int32, group_sta)[None, :]
    pick0 = (pair_sta[0][:, None] == sta_ids).astype(jnp.bfloat16)
    pick1 = (pair_sta[1][:, None] == sta_ids).astype(jnp.bfloat16)
    picks = jnp.concatenate([pick0, pick1], axis=0)
    assert lag_count % 2 == 1
    side = (lag_count - 1) // 2
    lag_pad = -(-(side + 1) // 128) * 128
    hi_all = angle_table(lax.iota(jnp.int32, total_bins // LOW) * LOW, lag_pad, total_bins)
    lo_all = angle_table(lax.iota(jnp.int32, LOW), lag_pad, total_bins)
    blocks = total_bins // FBLOCK
    assert total_bins % FBLOCK == 0
    lead = max(1, min(blocks - 1, (blocks * 31 + 25) // 50))
    bounds = [0, lead * FBLOCK, total_bins] if blocks > 1 else [0, total_bins]
    corr = jnp.zeros((pair_count, 2 * lag_pad), jnp.float32)
    for c in range(len(bounds) - 1):
        begin, end = bounds[c], bounds[c + 1]
        width = end - begin
        piece = whiten(spectra[:, :, begin:end]).reshape(spectra.shape[0], 2 * width)
        flat = lax.all_gather(piece, "sta", axis=0, tiled=True)
        if c:
            flat, corr = lax.optimization_barrier((flat, corr))
        both = jnp.dot(picks, flat, preferred_element_type=jnp.bfloat16)
        rows = slice(begin // LOW, end // LOW)
        tables = (hi_all[0][rows], hi_all[1][rows], lo_all[0], lo_all[1])
        corr = correlate(both, tables, corr)
    even = corr[:, : side + 1]
    odd = corr[:, lag_pad : lag_pad + side + 1]
    corr = jnp.concatenate([(even + odd)[:, :0:-1], even - odd], axis=1)
    corr = corr * jnp.float32(total_bins ** (-0.5)) * pair_valid.astype(jnp.float32)[:, None]
    lag_ext = -(-(lag_count + 1) // 128) * 128
    corr = jnp.concatenate(
        [corr, slot.astype(jnp.float32)[:, None], jnp.zeros((pair_count, lag_ext - lag_count - 1), jnp.float32)],
        axis=1,
    )
    dest = owner[:, 0]
    dest_hot = (dest[:, None] == lax.iota(jnp.int32, devices)[None, :]).astype(jnp.int32)
    before = jnp.cumsum(dest_hot, axis=0) - dest_hot
    position = jnp.sum(before * dest_hot, axis=1)
    flat = dest * capacity + position
    placing = (flat[:, None] == lax.iota(jnp.int32, devices * capacity)[None, :]).astype(
        jnp.float32
    )
    send_rows = jnp.dot(placing.T, corr, precision=lax.Precision.HIGHEST)
    got = lax.all_to_all(
        send_rows.reshape(devices, capacity, corr.shape[1]),
        ("grp", "sta"),
        split_axis=0,
        concat_axis=0,
        tiled=True,
    ).reshape(devices * capacity, corr.shape[1])
    got_rows = got[:, :lag_count]
    got_slots = got[:, lag_count]
    adding = (
        got_slots[None, :] == lax.iota(jnp.int32, stack_rows).astype(jnp.float32)[:, None]
    ).astype(jnp.float32)
    return stacks + jnp.dot(adding, got_rows, precision=lax.Precision.HIGHEST)


def solution(mesh):
    return jax.shard_map(
        local,
        mesh=mesh,
        in_specs=(
            P(("grp", "sta"), None, None),
            P(("grp", "sta"), None),
            P(None, ("grp", "sta")),
            P(("grp", "sta")),
            P(("grp", "sta"), None),
            P(("grp", "sta")),
        ),
        out_specs=P(("grp", "sta"), None),
        check_vma=False,
    )
```

```python
import math

import jax
import jax.numpy as jnp
from jax import lax
from jax.experimental import pallas as pl
from jax.experimental.pallas import tpu as pltpu
from jax.sharding import PartitionSpec as P

BAND = 64


def whiten(spectra):
    shape = spectra.shape
    split = spectra.reshape(shape[0], 2, shape[2] // BAND, BAND)
    power = jnp.mean(split * split, axis=(1, 3), keepdims=True)
    return (split * lax.rsqrt(power + 1e-06)).reshape(shape).astype(jnp.bfloat16)


def angle_table(freqs, lag_pad, total_bins):
    shifts = lax.iota(jnp.int32, lag_pad)
    angle_ids = jnp.mod(freqs[:, None] * shifts[None, :], 2 * total_bins)
    theta = angle_ids.astype(jnp.float32) * jnp.float32(math.pi / total_bins)
    return jnp.cos(theta), jnp.sin(theta)


LOW = 64
FBLOCK = 2048


def table_kernel(a0_ref, a1_ref, b0_ref, b1_ref, chi_ref, shi_ref, clo_ref, slo_ref, acc_ref, out_ref, ctab, stab):
    @pl.when(pl.program_id(0) == 0)
    def _():
        out_ref[...] = acc_ref[...]

    a0 = a0_ref[...].astype(jnp.float32)
    a1 = a1_ref[...].astype(jnp.float32)
    b0 = b0_ref[...].astype(jnp.float32)
    b1 = b1_ref[...].astype(jnp.float32)
    real = (a0 * b0 + a1 * b1).astype(jnp.bfloat16)
    imag = (a1 * b0 - a0 * b1).astype(jnp.bfloat16)

    def fill(j, carry):
        clo = clo_ref[...]
        slo = slo_ref[...]
        ch = chi_ref[pl.ds(j, 1), :]
        sh = shi_ref[pl.ds(j, 1), :]
        rows = pl.ds(pl.multiple_of(j * LOW, LOW), LOW)
        ctab[rows, :] = (ch * clo - sh * slo).astype(jnp.bfloat16)
        stab[rows, :] = (sh * clo + ch * slo).astype(jnp.bfloat16)
        return carry

    lax.fori_loop(0, FBLOCK // LOW, fill, 0)
    half = ctab.shape[1]
    out_ref[:, :half] += jnp.dot(real, ctab[...], preferred_element_type=jnp.float32)
    out_ref[:, half:] += jnp.dot(imag, stab[...], preferred_element_type=jnp.float32)


def correlate(both, tables, acc):
    cos_hi, sin_hi, cos_lo, sin_lo = tables
    pair_count = both.shape[0] // 2
    lag_pad = cos_lo.shape[1]
    width = both.shape[1] // 2
    hi_rows = FBLOCK // LOW
    assert width % FBLOCK == 0
    blocks = width // FBLOCK
    out = pl.pallas_call(
        table_kernel,
        grid=(blocks,),
        in_specs=[
            pl.BlockSpec((pair_count, FBLOCK), lambda i: (0, i)),
            pl.BlockSpec((pair_count, FBLOCK), lambda i: (0, i + blocks)),
            pl.BlockSpec((pair_count, FBLOCK), lambda i: (1, i)),
            pl.BlockSpec((pair_count, FBLOCK), lambda i: (1, i + blocks)),
            pl.BlockSpec((hi_rows, lag_pad), lambda i: (i, 0)),
            pl.BlockSpec((hi_rows, lag_pad), lambda i: (i, 0)),
            pl.BlockSpec((LOW, lag_pad), lambda i: (0, 0)),
            pl.BlockSpec((LOW, lag_pad), lambda i: (0, 0)),
            pl.BlockSpec((pair_count, 2 * lag_pad), lambda i: (0, 0)),
        ],
        out_specs=pl.BlockSpec((pair_count, 2 * lag_pad), lambda i: (0, 0)),
        out_shape=jax.ShapeDtypeStruct((pair_count, 2 * lag_pad), jnp.float32),
        scratch_shapes=[
            pltpu.VMEM((FBLOCK, lag_pad), jnp.bfloat16),
            pltpu.VMEM((FBLOCK, lag_pad), jnp.bfloat16),
        ],
        compiler_params=pltpu.CompilerParams(
            dimension_semantics=("arbitrary",), vmem_limit_bytes=48 * 1024 * 1024
        ),
        cost_estimate=pl.CostEstimate(
            flops=2 * 2 * pair_count * width * lag_pad + 10 * width * lag_pad,
            transcendentals=0,
            bytes_accessed=4 * pair_count * width * 2 + 4 * pair_count * lag_pad,
        ),
        input_output_aliases={8: 0},
    )(both, both, both, both, cos_hi, sin_hi, cos_lo, sin_lo, acc)
    return out


def local(spectra, stacks, pair_sta, pair_valid, owner, slot):
    total_bins = spectra.shape[2]
    lag_count = stacks.shape[1]
    stack_rows = stacks.shape[0]
    pair_count = pair_sta.shape[1]
    groups = lax.axis_size("grp")
    members = lax.axis_size("sta")
    devices = groups * members
    capacity = max(2, (4 * pair_count + 3 * devices - 1) // (3 * devices))
    group_sta = spectra.shape[0] * members
    sta_ids = lax.iota(jnp.int32, group_sta)[None, :]
    pick0 = (pair_sta[0][:, None] == sta_ids).astype(jnp.bfloat16)
    pick1 = (pair_sta[1][:, None] == sta_ids).astype(jnp.bfloat16)
    picks = jnp.concatenate([pick0, pick1], axis=0)
    assert lag_count % 2 == 1
    side = (lag_count - 1) // 2
    lag_pad = -(-(side + 1) // 128) * 128
    hi_all = angle_table(lax.iota(jnp.int32, total_bins // LOW) * LOW, lag_pad, total_bins)
    lo_all = angle_table(lax.iota(jnp.int32, LOW), lag_pad, total_bins)
    blocks = total_bins // FBLOCK
    assert total_bins % FBLOCK == 0
    lead = max(1, min(blocks - 1, (blocks * 57 + 50) // 100))
    bounds = [0, lead * FBLOCK, total_bins] if blocks > 1 else [0, total_bins]
    corr = jnp.zeros((pair_count, 2 * lag_pad), jnp.float32)
    for c in range(len(bounds) - 1):
        begin, end = bounds[c], bounds[c + 1]
        width = end - begin
        piece = whiten(spectra[:, :, begin:end]).reshape(spectra.shape[0], 2 * width)
        flat = lax.all_gather(piece, "sta", axis=0, tiled=True)
        if c:
            flat, corr = lax.optimization_barrier((flat, corr))
        both = jnp.dot(picks, flat, preferred_element_type=jnp.bfloat16)
        rows = slice(begin // LOW, end // LOW)
        tables = (hi_all[0][rows], hi_all[1][rows], lo_all[0], lo_all[1])
        corr = correlate(both, tables, corr)
    even = corr[:, : side + 1]
    odd = corr[:, lag_pad : lag_pad + side + 1]
    corr = jnp.concatenate([(even + odd)[:, :0:-1], even - odd], axis=1)
    corr = corr * jnp.float32(total_bins ** (-0.5)) * pair_valid.astype(jnp.float32)[:, None]
    lag_ext = -(-(lag_count + 1) // 128) * 128
    corr = jnp.concatenate(
        [corr, slot.astype(jnp.float32)[:, None], jnp.zeros((pair_count, lag_ext - lag_count - 1), jnp.float32)],
        axis=1,
    )
    dest = owner[:, 0]
    dest_hot = (dest[:, None] == lax.iota(jnp.int32, devices)[None, :]).astype(jnp.int32)
    before = jnp.cumsum(dest_hot, axis=0) - dest_hot
    position = jnp.sum(before * dest_hot, axis=1)
    flat = dest * capacity + position
    placing = (flat[:, None] == lax.iota(jnp.int32, devices * capacity)[None, :]).astype(
        jnp.float32
    )
    send_rows = jnp.dot(placing.T, corr, precision=lax.Precision.HIGHEST)
    got = lax.all_to_all(
        send_rows.reshape(devices, capacity, corr.shape[1]),
        ("grp", "sta"),
        split_axis=0,
        concat_axis=0,
        tiled=True,
    ).reshape(devices * capacity, corr.shape[1])
    got_rows = got[:, :lag_count]
    got_slots = got[:, lag_count]
    adding = (
        got_slots[None, :] == lax.iota(jnp.int32, stack_rows).astype(jnp.float32)[:, None]
    ).astype(jnp.float32)
    return stacks + jnp.dot(adding, got_rows, precision=lax.Precision.HIGHEST)


def solution(mesh):
    return jax.shard_map(
        local,
        mesh=mesh,
        in_specs=(
            P(("grp", "sta"), None, None),
            P(("grp", "sta"), None),
            P(None, ("grp", "sta")),
            P(("grp", "sta")),
            P(("grp", "sta"), None),
            P(("grp", "sta")),
        ),
        out_specs=P(("grp", "sta"), None),
        check_vma=False,
    )
```

```python
import math

import jax
import jax.numpy as jnp
from jax import lax
from jax.experimental import pallas as pl
from jax.experimental.pallas import tpu as pltpu
from jax.sharding import PartitionSpec as P

BAND = 64


def whiten(spectra):
    shape = spectra.shape
    split = spectra.reshape(shape[0], 2, shape[2] // BAND, BAND)
    power = jnp.mean(split * split, axis=(1, 3), keepdims=True)
    return (split * lax.rsqrt(power + 1e-06)).reshape(shape).astype(jnp.bfloat16)


def angle_table(freqs, lag_pad, total_bins):
    shifts = lax.iota(jnp.int32, lag_pad)
    angle_ids = jnp.mod(freqs[:, None] * shifts[None, :], 2 * total_bins)
    theta = angle_ids.astype(jnp.float32) * jnp.float32(math.pi / total_bins)
    return jnp.cos(theta), jnp.sin(theta)


LOW = 64
FBLOCK = 2048


def table_kernel(pick_ref, g0_ref, g1_ref, chi_ref, shi_ref, clo_ref, slo_ref, acc_ref, out_ref, ctab, stab):
    @pl.when(pl.program_id(0) == 0)
    def _():
        out_ref[...] = acc_ref[...]

    pairs = out_ref.shape[0]
    picks = pick_ref[...]
    rows0 = jnp.dot(picks, g0_ref[...], preferred_element_type=jnp.float32)
    rows1 = jnp.dot(picks, g1_ref[...], preferred_element_type=jnp.float32)
    a0 = rows0[:pairs]
    b0 = rows0[pairs:]
    a1 = rows1[:pairs]
    b1 = rows1[pairs:]
    real = (a0 * b0 + a1 * b1).astype(jnp.bfloat16)
    imag = (a1 * b0 - a0 * b1).astype(jnp.bfloat16)

    def fill(j, carry):
        clo = clo_ref[...]
        slo = slo_ref[...]
        ch = chi_ref[pl.ds(j, 1), :]
        sh = shi_ref[pl.ds(j, 1), :]
        rows = pl.ds(pl.multiple_of(j * LOW, LOW), LOW)
        ctab[rows, :] = (ch * clo - sh * slo).astype(jnp.bfloat16)
        stab[rows, :] = (sh * clo + ch * slo).astype(jnp.bfloat16)
        return carry

    lax.fori_loop(0, FBLOCK // LOW, fill, 0)
    half = ctab.shape[1]
    out_ref[:, :half] += jnp.dot(real, ctab[...], preferred_element_type=jnp.float32)
    out_ref[:, half:] += jnp.dot(imag, stab[...], preferred_element_type=jnp.float32)


def correlate(picks, flat, tables, acc):
    cos_hi, sin_hi, cos_lo, sin_lo = tables
    pair_count = picks.shape[0] // 2
    group_sta = flat.shape[0]
    lag_pad = cos_lo.shape[1]
    width = flat.shape[1] // 2
    hi_rows = FBLOCK // LOW
    assert width % FBLOCK == 0
    blocks = width // FBLOCK
    out = pl.pallas_call(
        table_kernel,
        grid=(blocks,),
        in_specs=[
            pl.BlockSpec((2 * pair_count, group_sta), lambda i: (0, 0)),
            pl.BlockSpec((group_sta, FBLOCK), lambda i: (0, i)),
            pl.BlockSpec((group_sta, FBLOCK), lambda i: (0, i + blocks)),
            pl.BlockSpec((hi_rows, lag_pad), lambda i: (i, 0)),
            pl.BlockSpec((hi_rows, lag_pad), lambda i: (i, 0)),
            pl.BlockSpec((LOW, lag_pad), lambda i: (0, 0)),
            pl.BlockSpec((LOW, lag_pad), lambda i: (0, 0)),
            pl.BlockSpec((pair_count, 2 * lag_pad), lambda i: (0, 0)),
        ],
        out_specs=pl.BlockSpec((pair_count, 2 * lag_pad), lambda i: (0, 0)),
        out_shape=jax.ShapeDtypeStruct((pair_count, 2 * lag_pad), jnp.float32),
        scratch_shapes=[
            pltpu.VMEM((FBLOCK, lag_pad), jnp.bfloat16),
            pltpu.VMEM((FBLOCK, lag_pad), jnp.bfloat16),
        ],
        compiler_params=pltpu.CompilerParams(
            dimension_semantics=("arbitrary",), vmem_limit_bytes=48 * 1024 * 1024
        ),
        cost_estimate=pl.CostEstimate(
            flops=2 * 2 * pair_count * width * lag_pad + 10 * width * lag_pad,
            transcendentals=0,
            bytes_accessed=4 * pair_count * width * 2 + 4 * pair_count * lag_pad,
        ),
        input_output_aliases={7: 0},
    )(picks, flat, flat, cos_hi, sin_hi, cos_lo, sin_lo, acc)
    return out


def local(spectra, stacks, pair_sta, pair_valid, owner, slot):
    total_bins = spectra.shape[2]
    lag_count = stacks.shape[1]
    stack_rows = stacks.shape[0]
    pair_count = pair_sta.shape[1]
    groups = lax.axis_size("grp")
    members = lax.axis_size("sta")
    devices = groups * members
    capacity = max(2, (4 * pair_count + 3 * devices - 1) // (3 * devices))
    group_sta = spectra.shape[0] * members
    sta_ids = lax.iota(jnp.int32, group_sta)[None, :]
    pick0 = (pair_sta[0][:, None] == sta_ids).astype(jnp.bfloat16)
    pick1 = (pair_sta[1][:, None] == sta_ids).astype(jnp.bfloat16)
    picks = jnp.concatenate([pick0, pick1], axis=0)
    assert lag_count % 2 == 1
    side = (lag_count - 1) // 2
    lag_pad = -(-(side + 1) // 128) * 128
    hi_all = angle_table(lax.iota(jnp.int32, total_bins // LOW) * LOW, lag_pad, total_bins)
    lo_all = angle_table(lax.iota(jnp.int32, LOW), lag_pad, total_bins)
    blocks = total_bins // FBLOCK
    assert total_bins % FBLOCK == 0
    lead = max(1, min(blocks - 1, (blocks * 57 + 50) // 100))
    bounds = [0, lead * FBLOCK, total_bins] if blocks > 1 else [0, total_bins]
    corr = jnp.zeros((pair_count, 2 * lag_pad), jnp.float32)
    for c in range(len(bounds) - 1):
        begin, end = bounds[c], bounds[c + 1]
        width = end - begin
        piece = whiten(spectra[:, :, begin:end]).reshape(spectra.shape[0], 2 * width)
        flat = lax.all_gather(piece, "sta", axis=0, tiled=True)
        if c:
            flat, corr = lax.optimization_barrier((flat, corr))
        rows = slice(begin // LOW, end // LOW)
        tables = (hi_all[0][rows], hi_all[1][rows], lo_all[0], lo_all[1])
        corr = correlate(picks, flat, tables, corr)
    even = corr[:, : side + 1]
    odd = corr[:, lag_pad : lag_pad + side + 1]
    corr = jnp.concatenate([(even + odd)[:, :0:-1], even - odd], axis=1)
    corr = corr * jnp.float32(total_bins ** (-0.5)) * pair_valid.astype(jnp.float32)[:, None]
    lag_ext = -(-(lag_count + 1) // 128) * 128
    corr = jnp.concatenate(
        [corr, slot.astype(jnp.float32)[:, None], jnp.zeros((pair_count, lag_ext - lag_count - 1), jnp.float32)],
        axis=1,
    )
    dest = owner[:, 0]
    dest_hot = (dest[:, None] == lax.iota(jnp.int32, devices)[None, :]).astype(jnp.int32)
    before = jnp.cumsum(dest_hot, axis=0) - dest_hot
    position = jnp.sum(before * dest_hot, axis=1)
    flat = dest * capacity + position
    placing = (flat[:, None] == lax.iota(jnp.int32, devices * capacity)[None, :]).astype(
        jnp.float32
    )
    send_rows = jnp.dot(placing.T, corr, precision=lax.Precision.HIGHEST)
    got = lax.all_to_all(
        send_rows.reshape(devices, capacity, corr.shape[1]),
        ("grp", "sta"),
        split_axis=0,
        concat_axis=0,
        tiled=True,
    ).reshape(devices * capacity, corr.shape[1])
    got_rows = got[:, :lag_count]
    got_slots = got[:, lag_count]
    adding = (
        got_slots[None, :] == lax.iota(jnp.int32, stack_rows).astype(jnp.float32)[:, None]
    ).astype(jnp.float32)
    return stacks + jnp.dot(adding, got_rows, precision=lax.Precision.HIGHEST)


def solution(mesh):
    return jax.shard_map(
        local,
        mesh=mesh,
        in_specs=(
            P(("grp", "sta"), None, None),
            P(("grp", "sta"), None),
            P(None, ("grp", "sta")),
            P(("grp", "sta")),
            P(("grp", "sta"), None),
            P(("grp", "sta")),
        ),
        out_specs=P(("grp", "sta"), None),
        check_vma=False,
    )
```

```python
import math

import jax
import jax.numpy as jnp
from jax import lax
from jax.experimental import pallas as pl
from jax.experimental.pallas import tpu as pltpu
from jax.sharding import PartitionSpec as P

BAND = 64


def whiten(spectra):
    shape = spectra.shape
    split = spectra.reshape(shape[0], 2, shape[2] // BAND, BAND)
    power = jnp.mean(split * split, axis=(1, 3), keepdims=True)
    return (split * lax.rsqrt(power + 1e-06)).reshape(shape).astype(jnp.bfloat16)


def angle_table(freqs, lag_pad, total_bins):
    shifts = lax.iota(jnp.int32, lag_pad)
    angle_ids = jnp.mod(freqs[:, None] * shifts[None, :], 2 * total_bins)
    theta = angle_ids.astype(jnp.float32) * jnp.float32(math.pi / total_bins)
    return jnp.cos(theta), jnp.sin(theta)


LOW = 64
FBLOCK = 2048


def table_kernel(pick_ref, g0_ref, g1_ref, chi_ref, shi_ref, clo_ref, slo_ref, acc_ref, out_ref, ctab, stab):
    @pl.when(pl.program_id(0) == 0)
    def _():
        out_ref[...] = acc_ref[...]

    pairs = out_ref.shape[0]
    picks = pick_ref[...]
    rows0 = jnp.dot(picks, g0_ref[...], preferred_element_type=jnp.float32)
    rows1 = jnp.dot(picks, g1_ref[...], preferred_element_type=jnp.float32)
    a0 = rows0[:pairs]
    b0 = rows0[pairs:]
    a1 = rows1[:pairs]
    b1 = rows1[pairs:]
    real = (a0 * b0 + a1 * b1).astype(jnp.bfloat16)
    imag = (a1 * b0 - a0 * b1).astype(jnp.bfloat16)

    def fill(j, carry):
        clo = clo_ref[...]
        slo = slo_ref[...]
        ch = chi_ref[pl.ds(j, 1), :]
        sh = shi_ref[pl.ds(j, 1), :]
        rows = pl.ds(pl.multiple_of(j * LOW, LOW), LOW)
        ctab[rows, :] = (ch * clo - sh * slo).astype(jnp.bfloat16)
        stab[rows, :] = (sh * clo + ch * slo).astype(jnp.bfloat16)
        return carry

    lax.fori_loop(0, FBLOCK // LOW, fill, 0)
    half = ctab.shape[1]
    out_ref[:, :half] += jnp.dot(real, ctab[...], preferred_element_type=jnp.float32)
    out_ref[:, half:] += jnp.dot(imag, stab[...], preferred_element_type=jnp.float32)


def correlate(picks, flat, tables, acc):
    cos_hi, sin_hi, cos_lo, sin_lo = tables
    pair_count = picks.shape[0] // 2
    group_sta = flat.shape[0]
    lag_pad = cos_lo.shape[1]
    width = flat.shape[1] // 2
    hi_rows = FBLOCK // LOW
    assert width % FBLOCK == 0
    blocks = width // FBLOCK
    out = pl.pallas_call(
        table_kernel,
        grid=(blocks,),
        in_specs=[
            pl.BlockSpec((2 * pair_count, group_sta), lambda i: (0, 0)),
            pl.BlockSpec((group_sta, FBLOCK), lambda i: (0, i)),
            pl.BlockSpec((group_sta, FBLOCK), lambda i: (0, i + blocks)),
            pl.BlockSpec((hi_rows, lag_pad), lambda i: (i, 0)),
            pl.BlockSpec((hi_rows, lag_pad), lambda i: (i, 0)),
            pl.BlockSpec((LOW, lag_pad), lambda i: (0, 0)),
            pl.BlockSpec((LOW, lag_pad), lambda i: (0, 0)),
            pl.BlockSpec((pair_count, 2 * lag_pad), lambda i: (0, 0)),
        ],
        out_specs=pl.BlockSpec((pair_count, 2 * lag_pad), lambda i: (0, 0)),
        out_shape=jax.ShapeDtypeStruct((pair_count, 2 * lag_pad), jnp.float32),
        scratch_shapes=[
            pltpu.VMEM((FBLOCK, lag_pad), jnp.bfloat16),
            pltpu.VMEM((FBLOCK, lag_pad), jnp.bfloat16),
        ],
        compiler_params=pltpu.CompilerParams(
            dimension_semantics=("arbitrary",), vmem_limit_bytes=48 * 1024 * 1024
        ),
        cost_estimate=pl.CostEstimate(
            flops=2 * 2 * pair_count * width * lag_pad + 10 * width * lag_pad,
            transcendentals=0,
            bytes_accessed=4 * pair_count * width * 2 + 4 * pair_count * lag_pad,
        ),
        input_output_aliases={7: 0},
    )(picks, flat, flat, cos_hi, sin_hi, cos_lo, sin_lo, acc)
    return out


def local(spectra, stacks, pair_sta, pair_valid, owner, slot):
    total_bins = spectra.shape[2]
    lag_count = stacks.shape[1]
    stack_rows = stacks.shape[0]
    pair_count = pair_sta.shape[1]
    groups = lax.axis_size("grp")
    members = lax.axis_size("sta")
    devices = groups * members
    capacity = max(2, (4 * pair_count + 3 * devices - 1) // (3 * devices))
    group_sta = spectra.shape[0] * members
    sta_ids = lax.iota(jnp.int32, group_sta)[None, :]
    pick0 = (pair_sta[0][:, None] == sta_ids).astype(jnp.bfloat16)
    pick1 = (pair_sta[1][:, None] == sta_ids).astype(jnp.bfloat16)
    picks = jnp.concatenate([pick0, pick1], axis=0)
    assert lag_count % 2 == 1
    side = (lag_count - 1) // 2
    lag_pad = -(-(side + 1) // 128) * 128
    hi_all = angle_table(lax.iota(jnp.int32, total_bins // LOW) * LOW, lag_pad, total_bins)
    lo_all = angle_table(lax.iota(jnp.int32, LOW), lag_pad, total_bins)
    blocks = total_bins // FBLOCK
    assert total_bins % FBLOCK == 0
    lead = max(1, min(blocks - 1, (2 * blocks + 1) // 3))
    bounds = [0, lead * FBLOCK, total_bins] if blocks > 1 else [0, total_bins]
    corr = jnp.zeros((pair_count, 2 * lag_pad), jnp.float32)
    for c in range(len(bounds) - 1):
        begin, end = bounds[c], bounds[c + 1]
        width = end - begin
        piece = whiten(spectra[:, :, begin:end]).reshape(spectra.shape[0], 2 * width)
        flat = lax.all_gather(piece, "sta", axis=0, tiled=True)
        if c:
            flat, corr = lax.optimization_barrier((flat, corr))
        rows = slice(begin // LOW, end // LOW)
        tables = (hi_all[0][rows], hi_all[1][rows], lo_all[0], lo_all[1])
        corr = correlate(picks, flat, tables, corr)
    even = corr[:, : side + 1]
    odd = corr[:, lag_pad : lag_pad + side + 1]
    corr = jnp.concatenate([(even + odd)[:, :0:-1], even - odd], axis=1)
    corr = corr * jnp.float32(total_bins ** (-0.5)) * pair_valid.astype(jnp.float32)[:, None]
    lag_ext = -(-(lag_count + 1) // 128) * 128
    corr = jnp.concatenate(
        [corr, slot.astype(jnp.float32)[:, None], jnp.zeros((pair_count, lag_ext - lag_count - 1), jnp.float32)],
        axis=1,
    )
    dest = owner[:, 0]
    dest_hot = (dest[:, None] == lax.iota(jnp.int32, devices)[None, :]).astype(jnp.int32)
    before = jnp.cumsum(dest_hot, axis=0) - dest_hot
    position = jnp.sum(before * dest_hot, axis=1)
    flat = dest * capacity + position
    placing = (flat[:, None] == lax.iota(jnp.int32, devices * capacity)[None, :]).astype(
        jnp.float32
    )
    send_rows = jnp.dot(placing.T, corr, precision=lax.Precision.HIGHEST)
    got = lax.all_to_all(
        send_rows.reshape(devices, capacity, corr.shape[1]),
        ("grp", "sta"),
        split_axis=0,
        concat_axis=0,
        tiled=True,
    ).reshape(devices * capacity, corr.shape[1])
    got_rows = got[:, :lag_count]
    got_slots = got[:, lag_count]
    adding = (
        got_slots[None, :] == lax.iota(jnp.int32, stack_rows).astype(jnp.float32)[:, None]
    ).astype(jnp.float32)
    return stacks + jnp.dot(adding, got_rows, precision=lax.Precision.HIGHEST)


def solution(mesh):
    return jax.shard_map(
        local,
        mesh=mesh,
        in_specs=(
            P(("grp", "sta"), None, None),
            P(("grp", "sta"), None),
            P(None, ("grp", "sta")),
            P(("grp", "sta")),
            P(("grp", "sta"), None),
            P(("grp", "sta")),
        ),
        out_specs=P(("grp", "sta"), None),
        check_vma=False,
    )
```

```python
import math

import jax
import jax.numpy as jnp
from jax import lax
from jax.experimental import pallas as pl
from jax.experimental.pallas import tpu as pltpu
from jax.sharding import PartitionSpec as P

BAND = 64


def whiten(spectra):
    shape = spectra.shape
    split = spectra.reshape(shape[0], 2, shape[2] // BAND, BAND)
    power = jnp.mean(split * split, axis=(1, 3), keepdims=True)
    return (split * lax.rsqrt(power + 1e-06)).reshape(shape).astype(jnp.bfloat16)


def angle_table(freqs, lag_pad, total_bins):
    shifts = lax.iota(jnp.int32, lag_pad)
    angle_ids = jnp.mod(freqs[:, None] * shifts[None, :], 2 * total_bins)
    theta = angle_ids.astype(jnp.float32) * jnp.float32(math.pi / total_bins)
    return jnp.cos(theta), jnp.sin(theta)


LOW = 64
FBLOCK = 2048


def table_kernel(pick_ref, g0_ref, g1_ref, chi_ref, shi_ref, clo_ref, slo_ref, acc_ref, out_ref, ctab, stab):
    @pl.when(pl.program_id(0) == 0)
    def _():
        out_ref[...] = acc_ref[...]

    pairs = out_ref.shape[0]
    picks = pick_ref[...]
    rows0 = jnp.dot(picks, g0_ref[...], preferred_element_type=jnp.float32)
    rows1 = jnp.dot(picks, g1_ref[...], preferred_element_type=jnp.float32)
    a0 = rows0[:pairs]
    b0 = rows0[pairs:]
    a1 = rows1[:pairs]
    b1 = rows1[pairs:]
    real = (a0 * b0 + a1 * b1).astype(jnp.bfloat16)
    imag = (a1 * b0 - a0 * b1).astype(jnp.bfloat16)

    def fill(j, carry):
        clo = clo_ref[...]
        slo = slo_ref[...]
        ch = chi_ref[pl.ds(j, 1), :]
        sh = shi_ref[pl.ds(j, 1), :]
        rows = pl.ds(pl.multiple_of(j * LOW, LOW), LOW)
        ctab[rows, :] = (ch * clo - sh * slo).astype(jnp.bfloat16)
        stab[rows, :] = (sh * clo + ch * slo).astype(jnp.bfloat16)
        return carry

    lax.fori_loop(0, FBLOCK // LOW, fill, 0)
    half = ctab.shape[1]
    out_ref[:, :half] += jnp.dot(real, ctab[...], preferred_element_type=jnp.float32)
    out_ref[:, half:] += jnp.dot(imag, stab[...], preferred_element_type=jnp.float32)


def fill_kernel(chi_ref, shi_ref, clo_ref, slo_ref, ctab, stab):
    def fill(j, carry):
        clo = clo_ref[...]
        slo = slo_ref[...]
        ch = chi_ref[pl.ds(j, 1), :]
        sh = shi_ref[pl.ds(j, 1), :]
        rows = pl.ds(pl.multiple_of(j * LOW, LOW), LOW)
        ctab[rows, :] = (ch * clo - sh * slo).astype(jnp.bfloat16)
        stab[rows, :] = (sh * clo + ch * slo).astype(jnp.bfloat16)
        return carry

    lax.fori_loop(0, FBLOCK // LOW, fill, 0)


def stored_kernel(pick_ref, g0_ref, g1_ref, ctab, stab, acc_ref, out_ref):
    @pl.when(pl.program_id(0) == 0)
    def _():
        out_ref[...] = acc_ref[...]

    pairs = out_ref.shape[0]
    picks = pick_ref[...]
    rows0 = jnp.dot(picks, g0_ref[...], preferred_element_type=jnp.float32)
    rows1 = jnp.dot(picks, g1_ref[...], preferred_element_type=jnp.float32)
    a0 = rows0[:pairs]
    b0 = rows0[pairs:]
    a1 = rows1[:pairs]
    b1 = rows1[pairs:]
    real = (a0 * b0 + a1 * b1).astype(jnp.bfloat16)
    imag = (a1 * b0 - a0 * b1).astype(jnp.bfloat16)
    half = ctab.shape[1]
    out_ref[:, :half] += jnp.dot(real, ctab[...], preferred_element_type=jnp.float32)
    out_ref[:, half:] += jnp.dot(imag, stab[...], preferred_element_type=jnp.float32)


def fill_tables(tables):
    cos_hi, sin_hi, cos_lo, sin_lo = tables
    lag_pad = cos_lo.shape[1]
    hi_rows = FBLOCK // LOW
    width = cos_hi.shape[0] * LOW
    blocks = width // FBLOCK
    spec = pl.BlockSpec((FBLOCK, lag_pad), lambda i: (i, 0))
    return pl.pallas_call(
        fill_kernel,
        grid=(blocks,),
        in_specs=[
            pl.BlockSpec((hi_rows, lag_pad), lambda i: (i, 0)),
            pl.BlockSpec((hi_rows, lag_pad), lambda i: (i, 0)),
            pl.BlockSpec((LOW, lag_pad), lambda i: (0, 0)),
            pl.BlockSpec((LOW, lag_pad), lambda i: (0, 0)),
        ],
        out_specs=[spec, spec],
        out_shape=[jax.ShapeDtypeStruct((width, lag_pad), jnp.bfloat16)] * 2,
        compiler_params=pltpu.CompilerParams(
            dimension_semantics=("arbitrary",), vmem_limit_bytes=48 * 1024 * 1024
        ),
        cost_estimate=pl.CostEstimate(
            flops=10 * width * lag_pad, transcendentals=0, bytes_accessed=4 * width * lag_pad
        ),
    )(cos_hi, sin_hi, cos_lo, sin_lo)


def correlate_stored(picks, flat, stored, acc):
    ctab, stab = stored
    pair_count = picks.shape[0] // 2
    group_sta = flat.shape[0]
    lag_pad = ctab.shape[1]
    width = flat.shape[1] // 2
    assert width % FBLOCK == 0 and ctab.shape[0] == width
    blocks = width // FBLOCK
    return pl.pallas_call(
        stored_kernel,
        grid=(blocks,),
        in_specs=[
            pl.BlockSpec((2 * pair_count, group_sta), lambda i: (0, 0)),
            pl.BlockSpec((group_sta, FBLOCK), lambda i: (0, i)),
            pl.BlockSpec((group_sta, FBLOCK), lambda i: (0, i + blocks)),
            pl.BlockSpec((FBLOCK, lag_pad), lambda i: (i, 0)),
            pl.BlockSpec((FBLOCK, lag_pad), lambda i: (i, 0)),
            pl.BlockSpec((pair_count, 2 * lag_pad), lambda i: (0, 0)),
        ],
        out_specs=pl.BlockSpec((pair_count, 2 * lag_pad), lambda i: (0, 0)),
        out_shape=jax.ShapeDtypeStruct((pair_count, 2 * lag_pad), jnp.float32),
        compiler_params=pltpu.CompilerParams(
            dimension_semantics=("arbitrary",), vmem_limit_bytes=48 * 1024 * 1024
        ),
        cost_estimate=pl.CostEstimate(
            flops=2 * 2 * pair_count * width * lag_pad,
            transcendentals=0,
            bytes_accessed=4 * width * lag_pad + 4 * pair_count * lag_pad,
        ),
        input_output_aliases={5: 0},
    )(picks, flat, flat, ctab, stab, acc)


def correlate(picks, flat, tables, acc):
    cos_hi, sin_hi, cos_lo, sin_lo = tables
    pair_count = picks.shape[0] // 2
    group_sta = flat.shape[0]
    lag_pad = cos_lo.shape[1]
    width = flat.shape[1] // 2
    hi_rows = FBLOCK // LOW
    assert width % FBLOCK == 0
    blocks = width // FBLOCK
    out = pl.pallas_call(
        table_kernel,
        grid=(blocks,),
        in_specs=[
            pl.BlockSpec((2 * pair_count, group_sta), lambda i: (0, 0)),
            pl.BlockSpec((group_sta, FBLOCK), lambda i: (0, i)),
            pl.BlockSpec((group_sta, FBLOCK), lambda i: (0, i + blocks)),
            pl.BlockSpec((hi_rows, lag_pad), lambda i: (i, 0)),
            pl.BlockSpec((hi_rows, lag_pad), lambda i: (i, 0)),
            pl.BlockSpec((LOW, lag_pad), lambda i: (0, 0)),
            pl.BlockSpec((LOW, lag_pad), lambda i: (0, 0)),
            pl.BlockSpec((pair_count, 2 * lag_pad), lambda i: (0, 0)),
        ],
        out_specs=pl.BlockSpec((pair_count, 2 * lag_pad), lambda i: (0, 0)),
        out_shape=jax.ShapeDtypeStruct((pair_count, 2 * lag_pad), jnp.float32),
        scratch_shapes=[
            pltpu.VMEM((FBLOCK, lag_pad), jnp.bfloat16),
            pltpu.VMEM((FBLOCK, lag_pad), jnp.bfloat16),
        ],
        compiler_params=pltpu.CompilerParams(
            dimension_semantics=("arbitrary",), vmem_limit_bytes=48 * 1024 * 1024
        ),
        cost_estimate=pl.CostEstimate(
            flops=2 * 2 * pair_count * width * lag_pad + 10 * width * lag_pad,
            transcendentals=0,
            bytes_accessed=4 * pair_count * width * 2 + 4 * pair_count * lag_pad,
        ),
        input_output_aliases={7: 0},
    )(picks, flat, flat, cos_hi, sin_hi, cos_lo, sin_lo, acc)
    return out


def local(spectra, stacks, pair_sta, pair_valid, owner, slot):
    total_bins = spectra.shape[2]
    lag_count = stacks.shape[1]
    stack_rows = stacks.shape[0]
    pair_count = pair_sta.shape[1]
    groups = lax.axis_size("grp")
    members = lax.axis_size("sta")
    devices = groups * members
    capacity = max(2, (4 * pair_count + 3 * devices - 1) // (3 * devices))
    group_sta = spectra.shape[0] * members
    sta_ids = lax.iota(jnp.int32, group_sta)[None, :]
    pick0 = (pair_sta[0][:, None] == sta_ids).astype(jnp.bfloat16)
    pick1 = (pair_sta[1][:, None] == sta_ids).astype(jnp.bfloat16)
    picks = jnp.concatenate([pick0, pick1], axis=0)
    assert lag_count % 2 == 1
    side = (lag_count - 1) // 2
    lag_pad = -(-(side + 1) // 128) * 128
    hi_all = angle_table(lax.iota(jnp.int32, total_bins // LOW) * LOW, lag_pad, total_bins)
    lo_all = angle_table(lax.iota(jnp.int32, LOW), lag_pad, total_bins)
    blocks = total_bins // FBLOCK
    assert total_bins % FBLOCK == 0
    lead = max(1, min(blocks - 1, (7 * blocks + 4) // 9))
    bounds = [0, lead * FBLOCK, total_bins] if blocks > 1 else [0, total_bins]
    corr = jnp.zeros((pair_count, 2 * lag_pad), jnp.float32)
    lead_rows = slice(0, bounds[1] // LOW)
    stored = fill_tables((hi_all[0][lead_rows], hi_all[1][lead_rows], lo_all[0], lo_all[1]))
    for c in range(len(bounds) - 1):
        begin, end = bounds[c], bounds[c + 1]
        width = end - begin
        piece = whiten(spectra[:, :, begin:end]).reshape(spectra.shape[0], 2 * width)
        flat = lax.all_gather(piece, "sta", axis=0, tiled=True)
        if c:
            flat, corr = lax.optimization_barrier((flat, corr))
        rows = slice(begin // LOW, end // LOW)
        tables = (hi_all[0][rows], hi_all[1][rows], lo_all[0], lo_all[1])
        if c == 0:
            corr = correlate_stored(picks, flat, stored, corr)
        else:
            corr = correlate(picks, flat, tables, corr)
    even = corr[:, : side + 1]
    odd = corr[:, lag_pad : lag_pad + side + 1]
    corr = jnp.concatenate([(even + odd)[:, :0:-1], even - odd], axis=1)
    corr = corr * jnp.float32(total_bins ** (-0.5)) * pair_valid.astype(jnp.float32)[:, None]
    lag_ext = -(-(lag_count + 1) // 128) * 128
    corr = jnp.concatenate(
        [corr, slot.astype(jnp.float32)[:, None], jnp.zeros((pair_count, lag_ext - lag_count - 1), jnp.float32)],
        axis=1,
    )
    dest = owner[:, 0]
    dest_hot = (dest[:, None] == lax.iota(jnp.int32, devices)[None, :]).astype(jnp.int32)
    before = jnp.cumsum(dest_hot, axis=0) - dest_hot
    position = jnp.sum(before * dest_hot, axis=1)
    flat = dest * capacity + position
    placing = (flat[:, None] == lax.iota(jnp.int32, devices * capacity)[None, :]).astype(
        jnp.float32
    )
    send_rows = jnp.dot(placing.T, corr, precision=lax.Precision.HIGHEST)
    got = lax.all_to_all(
        send_rows.reshape(devices, capacity, corr.shape[1]),
        ("grp", "sta"),
        split_axis=0,
        concat_axis=0,
        tiled=True,
    ).reshape(devices * capacity, corr.shape[1])
    got_rows = got[:, :lag_count]
    got_slots = got[:, lag_count]
    adding = (
        got_slots[None, :] == lax.iota(jnp.int32, stack_rows).astype(jnp.float32)[:, None]
    ).astype(jnp.float32)
    return stacks + jnp.dot(adding, got_rows, precision=lax.Precision.HIGHEST)


def solution(mesh):
    return jax.shard_map(
        local,
        mesh=mesh,
        in_specs=(
            P(("grp", "sta"), None, None),
            P(("grp", "sta"), None),
            P(None, ("grp", "sta")),
            P(("grp", "sta")),
            P(("grp", "sta"), None),
            P(("grp", "sta")),
        ),
        out_specs=P(("grp", "sta"), None),
        check_vma=False,
    )
```

```python
import math

import jax
import jax.numpy as jnp
from jax import lax
from jax.experimental import pallas as pl
from jax.experimental.pallas import tpu as pltpu
from jax.sharding import PartitionSpec as P

BAND = 64


def whiten(spectra):
    shape = spectra.shape
    split = spectra.reshape(shape[0], 2, shape[2] // BAND, BAND)
    power = jnp.mean(split * split, axis=(1, 3), keepdims=True)
    return (split * lax.rsqrt(power + 1e-06)).reshape(shape).astype(jnp.bfloat16)


def angle_table(freqs, lag_pad, total_bins):
    shifts = lax.iota(jnp.int32, lag_pad)
    angle_ids = jnp.mod(freqs[:, None] * shifts[None, :], 2 * total_bins)
    theta = angle_ids.astype(jnp.float32) * jnp.float32(math.pi / total_bins)
    return jnp.cos(theta), jnp.sin(theta)


LOW = 64
FBLOCK = 2048


def table_kernel(pick_ref, g0_ref, g1_ref, chi_ref, shi_ref, clo_ref, slo_ref, acc_ref, out_ref, ctab, stab):
    @pl.when(pl.program_id(0) == 0)
    def _():
        out_ref[...] = acc_ref[...]

    pairs = out_ref.shape[0]
    picks = pick_ref[...]
    rows0 = jnp.dot(picks, g0_ref[...], preferred_element_type=jnp.float32)
    rows1 = jnp.dot(picks, g1_ref[...], preferred_element_type=jnp.float32)
    a0 = rows0[:pairs]
    b0 = rows0[pairs:]
    a1 = rows1[:pairs]
    b1 = rows1[pairs:]
    real = (a0 * b0 + a1 * b1).astype(jnp.bfloat16)
    imag = (a1 * b0 - a0 * b1).astype(jnp.bfloat16)

    def fill(j, carry):
        clo = clo_ref[...]
        slo = slo_ref[...]
        ch = chi_ref[pl.ds(j, 1), :]
        sh = shi_ref[pl.ds(j, 1), :]
        rows = pl.ds(pl.multiple_of(j * LOW, LOW), LOW)
        ctab[rows, :] = (ch * clo - sh * slo).astype(jnp.bfloat16)
        stab[rows, :] = (sh * clo + ch * slo).astype(jnp.bfloat16)
        return carry

    lax.fori_loop(0, FBLOCK // LOW, fill, 0)
    half = ctab.shape[1]
    out_ref[:, :half] += jnp.dot(real, ctab[...], preferred_element_type=jnp.float32)
    out_ref[:, half:] += jnp.dot(imag, stab[...], preferred_element_type=jnp.float32)


def fill_kernel(chi_ref, shi_ref, clo_ref, slo_ref, ctab, stab):
    def fill(j, carry):
        clo = clo_ref[...]
        slo = slo_ref[...]
        ch = chi_ref[pl.ds(j, 1), :]
        sh = shi_ref[pl.ds(j, 1), :]
        rows = pl.ds(pl.multiple_of(j * LOW, LOW), LOW)
        ctab[rows, :] = (ch * clo - sh * slo).astype(jnp.bfloat16)
        stab[rows, :] = (sh * clo + ch * slo).astype(jnp.bfloat16)
        return carry

    lax.fori_loop(0, FBLOCK // LOW, fill, 0)


def stored_kernel(pick_ref, g0_ref, g1_ref, ctab, stab, acc_ref, out_ref):
    @pl.when(pl.program_id(0) == 0)
    def _():
        out_ref[...] = acc_ref[...]

    pairs = out_ref.shape[0]
    picks = pick_ref[...]
    rows0 = jnp.dot(picks, g0_ref[...], preferred_element_type=jnp.float32)
    rows1 = jnp.dot(picks, g1_ref[...], preferred_element_type=jnp.float32)
    a0 = rows0[:pairs]
    b0 = rows0[pairs:]
    a1 = rows1[:pairs]
    b1 = rows1[pairs:]
    real = (a0 * b0 + a1 * b1).astype(jnp.bfloat16)
    imag = (a1 * b0 - a0 * b1).astype(jnp.bfloat16)
    half = ctab.shape[1]
    out_ref[:, :half] += jnp.dot(real, ctab[...], preferred_element_type=jnp.float32)
    out_ref[:, half:] += jnp.dot(imag, stab[...], preferred_element_type=jnp.float32)


def fill_tables(tables):
    cos_hi, sin_hi, cos_lo, sin_lo = tables
    lag_pad = cos_lo.shape[1]
    hi_rows = FBLOCK // LOW
    width = cos_hi.shape[0] * LOW
    blocks = width // FBLOCK
    spec = pl.BlockSpec((FBLOCK, lag_pad), lambda i: (i, 0))
    return pl.pallas_call(
        fill_kernel,
        grid=(blocks,),
        in_specs=[
            pl.BlockSpec((hi_rows, lag_pad), lambda i: (i, 0)),
            pl.BlockSpec((hi_rows, lag_pad), lambda i: (i, 0)),
            pl.BlockSpec((LOW, lag_pad), lambda i: (0, 0)),
            pl.BlockSpec((LOW, lag_pad), lambda i: (0, 0)),
        ],
        out_specs=[spec, spec],
        out_shape=[jax.ShapeDtypeStruct((width, lag_pad), jnp.bfloat16)] * 2,
        compiler_params=pltpu.CompilerParams(
            dimension_semantics=("arbitrary",), vmem_limit_bytes=48 * 1024 * 1024
        ),
        cost_estimate=pl.CostEstimate(
            flops=10 * width * lag_pad, transcendentals=0, bytes_accessed=4 * width * lag_pad
        ),
    )(cos_hi, sin_hi, cos_lo, sin_lo)


def correlate_stored(picks, flat, stored, acc, begin):
    ctab, stab = stored
    pair_count = picks.shape[0] // 2
    group_sta = flat.shape[0]
    lag_pad = ctab.shape[1]
    width = flat.shape[1] // 2
    assert width % FBLOCK == 0 and begin % FBLOCK == 0
    blocks = width // FBLOCK
    skip = begin // FBLOCK
    return pl.pallas_call(
        stored_kernel,
        grid=(blocks,),
        in_specs=[
            pl.BlockSpec((2 * pair_count, group_sta), lambda i: (0, 0)),
            pl.BlockSpec((group_sta, FBLOCK), lambda i: (0, i)),
            pl.BlockSpec((group_sta, FBLOCK), lambda i: (0, i + blocks)),
            pl.BlockSpec((FBLOCK, lag_pad), lambda i: (i + skip, 0)),
            pl.BlockSpec((FBLOCK, lag_pad), lambda i: (i + skip, 0)),
            pl.BlockSpec((pair_count, 2 * lag_pad), lambda i: (0, 0)),
        ],
        out_specs=pl.BlockSpec((pair_count, 2 * lag_pad), lambda i: (0, 0)),
        out_shape=jax.ShapeDtypeStruct((pair_count, 2 * lag_pad), jnp.float32),
        compiler_params=pltpu.CompilerParams(
            dimension_semantics=("arbitrary",), vmem_limit_bytes=48 * 1024 * 1024
        ),
        cost_estimate=pl.CostEstimate(
            flops=2 * 2 * pair_count * width * lag_pad,
            transcendentals=0,
            bytes_accessed=4 * width * lag_pad + 4 * pair_count * lag_pad,
        ),
        input_output_aliases={5: 0},
    )(picks, flat, flat, ctab, stab, acc)


def correlate(picks, flat, tables, acc):
    cos_hi, sin_hi, cos_lo, sin_lo = tables
    pair_count = picks.shape[0] // 2
    group_sta = flat.shape[0]
    lag_pad = cos_lo.shape[1]
    width = flat.shape[1] // 2
    hi_rows = FBLOCK // LOW
    assert width % FBLOCK == 0
    blocks = width // FBLOCK
    out = pl.pallas_call(
        table_kernel,
        grid=(blocks,),
        in_specs=[
            pl.BlockSpec((2 * pair_count, group_sta), lambda i: (0, 0)),
            pl.BlockSpec((group_sta, FBLOCK), lambda i: (0, i)),
            pl.BlockSpec((group_sta, FBLOCK), lambda i: (0, i + blocks)),
            pl.BlockSpec((hi_rows, lag_pad), lambda i: (i, 0)),
            pl.BlockSpec((hi_rows, lag_pad), lambda i: (i, 0)),
            pl.BlockSpec((LOW, lag_pad), lambda i: (0, 0)),
            pl.BlockSpec((LOW, lag_pad), lambda i: (0, 0)),
            pl.BlockSpec((pair_count, 2 * lag_pad), lambda i: (0, 0)),
        ],
        out_specs=pl.BlockSpec((pair_count, 2 * lag_pad), lambda i: (0, 0)),
        out_shape=jax.ShapeDtypeStruct((pair_count, 2 * lag_pad), jnp.float32),
        scratch_shapes=[
            pltpu.VMEM((FBLOCK, lag_pad), jnp.bfloat16),
            pltpu.VMEM((FBLOCK, lag_pad), jnp.bfloat16),
        ],
        compiler_params=pltpu.CompilerParams(
            dimension_semantics=("arbitrary",), vmem_limit_bytes=48 * 1024 * 1024
        ),
        cost_estimate=pl.CostEstimate(
            flops=2 * 2 * pair_count * width * lag_pad + 10 * width * lag_pad,
            transcendentals=0,
            bytes_accessed=4 * pair_count * width * 2 + 4 * pair_count * lag_pad,
        ),
        input_output_aliases={7: 0},
    )(picks, flat, flat, cos_hi, sin_hi, cos_lo, sin_lo, acc)
    return out


def local(spectra, stacks, pair_sta, pair_valid, owner, slot):
    total_bins = spectra.shape[2]
    lag_count = stacks.shape[1]
    stack_rows = stacks.shape[0]
    pair_count = pair_sta.shape[1]
    groups = lax.axis_size("grp")
    members = lax.axis_size("sta")
    devices = groups * members
    capacity = max(2, (4 * pair_count + 3 * devices - 1) // (3 * devices))
    group_sta = spectra.shape[0] * members
    sta_ids = lax.iota(jnp.int32, group_sta)[None, :]
    pick0 = (pair_sta[0][:, None] == sta_ids).astype(jnp.bfloat16)
    pick1 = (pair_sta[1][:, None] == sta_ids).astype(jnp.bfloat16)
    picks = jnp.concatenate([pick0, pick1], axis=0)
    assert lag_count % 2 == 1
    side = (lag_count - 1) // 2
    lag_pad = -(-(side + 1) // 128) * 128
    hi_all = angle_table(lax.iota(jnp.int32, total_bins // LOW) * LOW, lag_pad, total_bins)
    lo_all = angle_table(lax.iota(jnp.int32, LOW), lag_pad, total_bins)
    blocks = total_bins // FBLOCK
    assert total_bins % FBLOCK == 0
    lead = max(1, min(blocks - 1, (7 * blocks + 4) // 9))
    bounds = [0, lead * FBLOCK, total_bins] if blocks > 1 else [0, total_bins]
    corr = jnp.zeros((pair_count, 2 * lag_pad), jnp.float32)
    stored = fill_tables((hi_all[0], hi_all[1], lo_all[0], lo_all[1]))
    for c in range(len(bounds) - 1):
        begin, end = bounds[c], bounds[c + 1]
        width = end - begin
        piece = whiten(spectra[:, :, begin:end]).reshape(spectra.shape[0], 2 * width)
        flat = lax.all_gather(piece, "sta", axis=0, tiled=True)
        if c:
            flat, corr = lax.optimization_barrier((flat, corr))
        corr = correlate_stored(picks, flat, stored, corr, begin)
    even = corr[:, : side + 1]
    odd = corr[:, lag_pad : lag_pad + side + 1]
    corr = jnp.concatenate([(even + odd)[:, :0:-1], even - odd], axis=1)
    corr = corr * jnp.float32(total_bins ** (-0.5)) * pair_valid.astype(jnp.float32)[:, None]
    lag_ext = -(-(lag_count + 1) // 128) * 128
    corr = jnp.concatenate(
        [corr, slot.astype(jnp.float32)[:, None], jnp.zeros((pair_count, lag_ext - lag_count - 1), jnp.float32)],
        axis=1,
    )
    dest = owner[:, 0]
    dest_hot = (dest[:, None] == lax.iota(jnp.int32, devices)[None, :]).astype(jnp.int32)
    before = jnp.cumsum(dest_hot, axis=0) - dest_hot
    position = jnp.sum(before * dest_hot, axis=1)
    flat = dest * capacity + position
    placing = (flat[:, None] == lax.iota(jnp.int32, devices * capacity)[None, :]).astype(
        jnp.float32
    )
    send_rows = jnp.dot(placing.T, corr, precision=lax.Precision.HIGHEST)
    got = lax.all_to_all(
        send_rows.reshape(devices, capacity, corr.shape[1]),
        ("grp", "sta"),
        split_axis=0,
        concat_axis=0,
        tiled=True,
    ).reshape(devices * capacity, corr.shape[1])
    got_rows = got[:, :lag_count]
    got_slots = got[:, lag_count]
    adding = (
        got_slots[None, :] == lax.iota(jnp.int32, stack_rows).astype(jnp.float32)[:, None]
    ).astype(jnp.float32)
    return stacks + jnp.dot(adding, got_rows, precision=lax.Precision.HIGHEST)


def solution(mesh):
    return jax.shard_map(
        local,
        mesh=mesh,
        in_specs=(
            P(("grp", "sta"), None, None),
            P(("grp", "sta"), None),
            P(None, ("grp", "sta")),
            P(("grp", "sta")),
            P(("grp", "sta"), None),
            P(("grp", "sta")),
        ),
        out_specs=P(("grp", "sta"), None),
        check_vma=False,
    )
```

```python
import math

import jax
import jax.numpy as jnp
from jax import lax
from jax.experimental import pallas as pl
from jax.experimental.pallas import tpu as pltpu
from jax.sharding import PartitionSpec as P

BAND = 64


def whiten(spectra):
    shape = spectra.shape
    split = spectra.reshape(shape[0], 2, shape[2] // BAND, BAND)
    power = jnp.mean(split * split, axis=(1, 3), keepdims=True)
    return (split * lax.rsqrt(power + 1e-06)).reshape(shape).astype(jnp.bfloat16)


def angle_table(freqs, lag_pad, total_bins):
    shifts = lax.iota(jnp.int32, lag_pad)
    angle_ids = jnp.mod(freqs[:, None] * shifts[None, :], 2 * total_bins)
    theta = angle_ids.astype(jnp.float32) * jnp.float32(math.pi / total_bins)
    return jnp.cos(theta), jnp.sin(theta)


LOW = 64
FBLOCK = 2048


def table_kernel(pick_ref, g0_ref, g1_ref, chi_ref, shi_ref, clo_ref, slo_ref, acc_ref, out_ref, ctab, stab):
    @pl.when(pl.program_id(0) == 0)
    def _():
        out_ref[...] = acc_ref[...]

    pairs = out_ref.shape[0]
    picks = pick_ref[...]
    rows0 = jnp.dot(picks, g0_ref[...], preferred_element_type=jnp.float32)
    rows1 = jnp.dot(picks, g1_ref[...], preferred_element_type=jnp.float32)
    a0 = rows0[:pairs]
    b0 = rows0[pairs:]
    a1 = rows1[:pairs]
    b1 = rows1[pairs:]
    real = (a0 * b0 + a1 * b1).astype(jnp.bfloat16)
    imag = (a1 * b0 - a0 * b1).astype(jnp.bfloat16)

    def fill(j, carry):
        clo = clo_ref[...]
        slo = slo_ref[...]
        ch = chi_ref[pl.ds(j, 1), :]
        sh = shi_ref[pl.ds(j, 1), :]
        rows = pl.ds(pl.multiple_of(j * LOW, LOW), LOW)
        ctab[rows, :] = (ch * clo - sh * slo).astype(jnp.bfloat16)
        stab[rows, :] = (sh * clo + ch * slo).astype(jnp.bfloat16)
        return carry

    lax.fori_loop(0, FBLOCK // LOW, fill, 0)
    half = ctab.shape[1]
    out_ref[:, :half] += jnp.dot(real, ctab[...], preferred_element_type=jnp.float32)
    out_ref[:, half:] += jnp.dot(imag, stab[...], preferred_element_type=jnp.float32)


def fill_kernel(chi_ref, shi_ref, clo_ref, slo_ref, ctab, stab):
    def fill(j, carry):
        clo = clo_ref[...]
        slo = slo_ref[...]
        ch = chi_ref[pl.ds(j, 1), :]
        sh = shi_ref[pl.ds(j, 1), :]
        rows = pl.ds(pl.multiple_of(j * LOW, LOW), LOW)
        ctab[rows, :] = (ch * clo - sh * slo).astype(jnp.bfloat16)
        stab[rows, :] = (sh * clo + ch * slo).astype(jnp.bfloat16)
        return carry

    lax.fori_loop(0, FBLOCK // LOW, fill, 0)


def stored_kernel(pick_ref, g0_ref, g1_ref, ctab, stab, acc_ref, out_ref):
    @pl.when(pl.program_id(0) == 0)
    def _():
        out_ref[...] = acc_ref[...]

    pairs = out_ref.shape[0]
    picks = pick_ref[...]
    rows0 = jnp.dot(picks, g0_ref[...], preferred_element_type=jnp.float32)
    rows1 = jnp.dot(picks, g1_ref[...], preferred_element_type=jnp.float32)
    a0 = rows0[:pairs]
    b0 = rows0[pairs:]
    a1 = rows1[:pairs]
    b1 = rows1[pairs:]
    real = (a0 * b0 + a1 * b1).astype(jnp.bfloat16)
    imag = (a1 * b0 - a0 * b1).astype(jnp.bfloat16)
    half = ctab.shape[1]
    out_ref[:, :half] += jnp.dot(real, ctab[...], preferred_element_type=jnp.float32)
    out_ref[:, half:] += jnp.dot(imag, stab[...], preferred_element_type=jnp.float32)


def fill_tables(tables):
    cos_hi, sin_hi, cos_lo, sin_lo = tables
    lag_pad = cos_lo.shape[1]
    hi_rows = FBLOCK // LOW
    width = cos_hi.shape[0] * LOW
    blocks = width // FBLOCK
    spec = pl.BlockSpec((FBLOCK, lag_pad), lambda i: (i, 0))
    return pl.pallas_call(
        fill_kernel,
        grid=(blocks,),
        in_specs=[
            pl.BlockSpec((hi_rows, lag_pad), lambda i: (i, 0)),
            pl.BlockSpec((hi_rows, lag_pad), lambda i: (i, 0)),
            pl.BlockSpec((LOW, lag_pad), lambda i: (0, 0)),
            pl.BlockSpec((LOW, lag_pad), lambda i: (0, 0)),
        ],
        out_specs=[spec, spec],
        out_shape=[jax.ShapeDtypeStruct((width, lag_pad), jnp.bfloat16)] * 2,
        compiler_params=pltpu.CompilerParams(
            dimension_semantics=("arbitrary",), vmem_limit_bytes=48 * 1024 * 1024
        ),
        cost_estimate=pl.CostEstimate(
            flops=10 * width * lag_pad, transcendentals=0, bytes_accessed=4 * width * lag_pad
        ),
    )(cos_hi, sin_hi, cos_lo, sin_lo)


def correlate_stored(picks, flat, stored, acc, begin):
    ctab, stab = stored
    pair_count = picks.shape[0] // 2
    group_sta = flat.shape[0]
    lag_pad = ctab.shape[1]
    width = flat.shape[1] // 2
    assert width % FBLOCK == 0 and begin % FBLOCK == 0
    blocks = width // FBLOCK
    skip = begin // FBLOCK
    return pl.pallas_call(
        stored_kernel,
        grid=(blocks,),
        in_specs=[
            pl.BlockSpec((2 * pair_count, group_sta), lambda i: (0, 0)),
            pl.BlockSpec((group_sta, FBLOCK), lambda i: (0, i)),
            pl.BlockSpec((group_sta, FBLOCK), lambda i: (0, i + blocks)),
            pl.BlockSpec((FBLOCK, lag_pad), lambda i: (i + skip, 0)),
            pl.BlockSpec((FBLOCK, lag_pad), lambda i: (i + skip, 0)),
            pl.BlockSpec((pair_count, 2 * lag_pad), lambda i: (0, 0)),
        ],
        out_specs=pl.BlockSpec((pair_count, 2 * lag_pad), lambda i: (0, 0)),
        out_shape=jax.ShapeDtypeStruct((pair_count, 2 * lag_pad), jnp.float32),
        compiler_params=pltpu.CompilerParams(
            dimension_semantics=("arbitrary",), vmem_limit_bytes=48 * 1024 * 1024
        ),
        cost_estimate=pl.CostEstimate(
            flops=2 * 2 * pair_count * width * lag_pad,
            transcendentals=0,
            bytes_accessed=4 * width * lag_pad + 4 * pair_count * lag_pad,
        ),
        input_output_aliases={5: 0},
    )(picks, flat, flat, ctab, stab, acc)


def correlate(picks, flat, tables, acc):
    cos_hi, sin_hi, cos_lo, sin_lo = tables
    pair_count = picks.shape[0] // 2
    group_sta = flat.shape[0]
    lag_pad = cos_lo.shape[1]
    width = flat.shape[1] // 2
    hi_rows = FBLOCK // LOW
    assert width % FBLOCK == 0
    blocks = width // FBLOCK
    out = pl.pallas_call(
        table_kernel,
        grid=(blocks,),
        in_specs=[
            pl.BlockSpec((2 * pair_count, group_sta), lambda i: (0, 0)),
            pl.BlockSpec((group_sta, FBLOCK), lambda i: (0, i)),
            pl.BlockSpec((group_sta, FBLOCK), lambda i: (0, i + blocks)),
            pl.BlockSpec((hi_rows, lag_pad), lambda i: (i, 0)),
            pl.BlockSpec((hi_rows, lag_pad), lambda i: (i, 0)),
            pl.BlockSpec((LOW, lag_pad), lambda i: (0, 0)),
            pl.BlockSpec((LOW, lag_pad), lambda i: (0, 0)),
            pl.BlockSpec((pair_count, 2 * lag_pad), lambda i: (0, 0)),
        ],
        out_specs=pl.BlockSpec((pair_count, 2 * lag_pad), lambda i: (0, 0)),
        out_shape=jax.ShapeDtypeStruct((pair_count, 2 * lag_pad), jnp.float32),
        scratch_shapes=[
            pltpu.VMEM((FBLOCK, lag_pad), jnp.bfloat16),
            pltpu.VMEM((FBLOCK, lag_pad), jnp.bfloat16),
        ],
        compiler_params=pltpu.CompilerParams(
            dimension_semantics=("arbitrary",), vmem_limit_bytes=48 * 1024 * 1024
        ),
        cost_estimate=pl.CostEstimate(
            flops=2 * 2 * pair_count * width * lag_pad + 10 * width * lag_pad,
            transcendentals=0,
            bytes_accessed=4 * pair_count * width * 2 + 4 * pair_count * lag_pad,
        ),
        input_output_aliases={7: 0},
    )(picks, flat, flat, cos_hi, sin_hi, cos_lo, sin_lo, acc)
    return out


def local(spectra, stacks, pair_sta, pair_valid, owner, slot):
    total_bins = spectra.shape[2]
    lag_count = stacks.shape[1]
    stack_rows = stacks.shape[0]
    pair_count = pair_sta.shape[1]
    groups = lax.axis_size("grp")
    members = lax.axis_size("sta")
    devices = groups * members
    capacity = max(2, (4 * pair_count + 3 * devices - 1) // (3 * devices))
    group_sta = spectra.shape[0] * members
    sta_ids = lax.iota(jnp.int32, group_sta)[None, :]
    pick0 = (pair_sta[0][:, None] == sta_ids).astype(jnp.bfloat16)
    pick1 = (pair_sta[1][:, None] == sta_ids).astype(jnp.bfloat16)
    picks = jnp.concatenate([pick0, pick1], axis=0)
    assert lag_count % 2 == 1
    side = (lag_count - 1) // 2
    lag_pad = -(-(side + 1) // 128) * 128
    hi_all = angle_table(lax.iota(jnp.int32, total_bins // LOW) * LOW, lag_pad, total_bins)
    lo_all = angle_table(lax.iota(jnp.int32, LOW), lag_pad, total_bins)
    blocks = total_bins // FBLOCK
    assert total_bins % FBLOCK == 0
    lead = max(1, min(blocks - 1, (7 * blocks + 4) // 9))
    bounds = [0, lead * FBLOCK, total_bins] if blocks > 1 else [0, total_bins]
    corr = jnp.zeros((pair_count, 2 * lag_pad), jnp.float32)
    stored = fill_tables((hi_all[0], hi_all[1], lo_all[0], lo_all[1]))
    for c in range(len(bounds) - 1):
        begin, end = bounds[c], bounds[c + 1]
        width = end - begin
        piece = whiten(spectra[:, :, begin:end]).reshape(spectra.shape[0], 2 * width)
        flat = lax.all_gather(piece, "sta", axis=0, tiled=True)
        if c:
            flat, corr = lax.optimization_barrier((flat, corr))
        corr = correlate_stored(picks, flat, stored, corr, begin)
    even = corr[:, : side + 1]
    odd = corr[:, lag_pad : lag_pad + side + 1]
    corr = jnp.concatenate([(even + odd)[:, :0:-1], even - odd], axis=1)
    corr = corr * jnp.float32(total_bins ** (-0.5)) * pair_valid.astype(jnp.float32)[:, None]
    lag_ext = -(-(lag_count + 1) // 128) * 128
    corr = jnp.concatenate(
        [corr, slot.astype(jnp.float32)[:, None], jnp.zeros((pair_count, lag_ext - lag_count - 1), jnp.float32)],
        axis=1,
    )
    dest = owner[:, 0]
    dest_hot = (dest[:, None] == lax.iota(jnp.int32, devices)[None, :]).astype(jnp.int32)
    before = jnp.cumsum(dest_hot, axis=0) - dest_hot
    position = jnp.sum(before * dest_hot, axis=1)
    flat = dest * capacity + position
    placing = (flat[:, None] == lax.iota(jnp.int32, devices * capacity)[None, :]).astype(
        jnp.float32
    )
    send_rows = jnp.dot(placing.T, corr, precision=lax.Precision.HIGHEST)
    got = lax.all_to_all(
        send_rows.reshape(devices, capacity * corr.shape[1]),
        ("grp", "sta"),
        split_axis=0,
        concat_axis=0,
        tiled=True,
    ).reshape(devices * capacity, corr.shape[1])
    got_rows = got[:, :lag_count]
    got_slots = got[:, lag_count]
    adding = (
        got_slots[None, :] == lax.iota(jnp.int32, stack_rows).astype(jnp.float32)[:, None]
    ).astype(jnp.float32)
    return stacks + jnp.dot(adding, got_rows, precision=lax.Precision.HIGHEST)


def solution(mesh):
    return jax.shard_map(
        local,
        mesh=mesh,
        in_specs=(
            P(("grp", "sta"), None, None),
            P(("grp", "sta"), None),
            P(None, ("grp", "sta")),
            P(("grp", "sta")),
            P(("grp", "sta"), None),
            P(("grp", "sta")),
        ),
        out_specs=P(("grp", "sta"), None),
        check_vma=False,
    )
```

```python
import math

import jax
import jax.numpy as jnp
from jax import lax
from jax.experimental import pallas as pl
from jax.experimental.pallas import tpu as pltpu
from jax.sharding import PartitionSpec as P

BAND = 64


def whiten(spectra):
    shape = spectra.shape
    split = spectra.reshape(shape[0], 2, shape[2] // BAND, BAND)
    power = jnp.mean(split * split, axis=(1, 3), keepdims=True)
    return (split * lax.rsqrt(power + 1e-06)).reshape(shape).astype(jnp.bfloat16)


def angle_table(freqs, lag_pad, total_bins):
    shifts = lax.iota(jnp.int32, lag_pad)
    angle_ids = jnp.mod(freqs[:, None] * shifts[None, :], 2 * total_bins)
    theta = angle_ids.astype(jnp.float32) * jnp.float32(math.pi / total_bins)
    return jnp.cos(theta), jnp.sin(theta)


LOW = 64
FBLOCK = 2048


def table_kernel(pick_ref, g0_ref, g1_ref, chi_ref, shi_ref, clo_ref, slo_ref, acc_ref, out_ref, ctab, stab):
    @pl.when(pl.program_id(0) == 0)
    def _():
        out_ref[...] = acc_ref[...]

    pairs = out_ref.shape[0]
    picks = pick_ref[...]
    rows0 = jnp.dot(picks, g0_ref[...], preferred_element_type=jnp.float32)
    rows1 = jnp.dot(picks, g1_ref[...], preferred_element_type=jnp.float32)
    a0 = rows0[:pairs]
    b0 = rows0[pairs:]
    a1 = rows1[:pairs]
    b1 = rows1[pairs:]
    real = (a0 * b0 + a1 * b1).astype(jnp.bfloat16)
    imag = (a1 * b0 - a0 * b1).astype(jnp.bfloat16)

    def fill(j, carry):
        clo = clo_ref[...]
        slo = slo_ref[...]
        ch = chi_ref[pl.ds(j, 1), :]
        sh = shi_ref[pl.ds(j, 1), :]
        rows = pl.ds(pl.multiple_of(j * LOW, LOW), LOW)
        ctab[rows, :] = (ch * clo - sh * slo).astype(jnp.bfloat16)
        stab[rows, :] = (sh * clo + ch * slo).astype(jnp.bfloat16)
        return carry

    lax.fori_loop(0, FBLOCK // LOW, fill, 0)
    half = ctab.shape[1]
    out_ref[:, :half] += jnp.dot(real, ctab[...], preferred_element_type=jnp.float32)
    out_ref[:, half:] += jnp.dot(imag, stab[...], preferred_element_type=jnp.float32)


def fill_kernel(chi_ref, shi_ref, clo_ref, slo_ref, ctab, stab):
    def fill(j, carry):
        clo = clo_ref[...]
        slo = slo_ref[...]
        ch = chi_ref[pl.ds(j, 1), :]
        sh = shi_ref[pl.ds(j, 1), :]
        rows = pl.ds(pl.multiple_of(j * LOW, LOW), LOW)
        ctab[rows, :] = (ch * clo - sh * slo).astype(jnp.bfloat16)
        stab[rows, :] = (sh * clo + ch * slo).astype(jnp.bfloat16)
        return carry

    lax.fori_loop(0, FBLOCK // LOW, fill, 0)


def stored_kernel(pick_ref, g0_ref, g1_ref, ctab, stab, acc_ref, out_ref):
    @pl.when(pl.program_id(0) == 0)
    def _():
        out_ref[...] = acc_ref[...]

    pairs = out_ref.shape[0]
    picks = pick_ref[...]
    rows0 = jnp.dot(picks, g0_ref[...], preferred_element_type=jnp.float32)
    rows1 = jnp.dot(picks, g1_ref[...], preferred_element_type=jnp.float32)
    a0 = rows0[:pairs]
    b0 = rows0[pairs:]
    a1 = rows1[:pairs]
    b1 = rows1[pairs:]
    real = (a0 * b0 + a1 * b1).astype(jnp.bfloat16)
    imag = (a1 * b0 - a0 * b1).astype(jnp.bfloat16)
    half = ctab.shape[1]
    out_ref[:, :half] += jnp.dot(real, ctab[...], preferred_element_type=jnp.float32)
    out_ref[:, half:] += jnp.dot(imag, stab[...], preferred_element_type=jnp.float32)


def fill_tables(tables):
    cos_hi, sin_hi, cos_lo, sin_lo = tables
    lag_pad = cos_lo.shape[1]
    hi_rows = FBLOCK // LOW
    width = cos_hi.shape[0] * LOW
    blocks = width // FBLOCK
    spec = pl.BlockSpec((FBLOCK, lag_pad), lambda i: (i, 0))
    return pl.pallas_call(
        fill_kernel,
        grid=(blocks,),
        in_specs=[
            pl.BlockSpec((hi_rows, lag_pad), lambda i: (i, 0)),
            pl.BlockSpec((hi_rows, lag_pad), lambda i: (i, 0)),
            pl.BlockSpec((LOW, lag_pad), lambda i: (0, 0)),
            pl.BlockSpec((LOW, lag_pad), lambda i: (0, 0)),
        ],
        out_specs=[spec, spec],
        out_shape=[jax.ShapeDtypeStruct((width, lag_pad), jnp.bfloat16)] * 2,
        compiler_params=pltpu.CompilerParams(
            dimension_semantics=("arbitrary",), vmem_limit_bytes=48 * 1024 * 1024
        ),
        cost_estimate=pl.CostEstimate(
            flops=10 * width * lag_pad, transcendentals=0, bytes_accessed=4 * width * lag_pad
        ),
    )(cos_hi, sin_hi, cos_lo, sin_lo)


def correlate_stored(picks, flat, stored, acc, begin):
    ctab, stab = stored
    pair_count = picks.shape[0] // 2
    group_sta = flat.shape[0]
    lag_pad = ctab.shape[1]
    width = flat.shape[1] // 2
    assert width % FBLOCK == 0 and begin % FBLOCK == 0
    blocks = width // FBLOCK
    skip = begin // FBLOCK
    return pl.pallas_call(
        stored_kernel,
        grid=(blocks,),
        in_specs=[
            pl.BlockSpec((2 * pair_count, group_sta), lambda i: (0, 0)),
            pl.BlockSpec((group_sta, FBLOCK), lambda i: (0, i)),
            pl.BlockSpec((group_sta, FBLOCK), lambda i: (0, i + blocks)),
            pl.BlockSpec((FBLOCK, lag_pad), lambda i: (i + skip, 0)),
            pl.BlockSpec((FBLOCK, lag_pad), lambda i: (i + skip, 0)),
            pl.BlockSpec((pair_count, 2 * lag_pad), lambda i: (0, 0)),
        ],
        out_specs=pl.BlockSpec((pair_count, 2 * lag_pad), lambda i: (0, 0)),
        out_shape=jax.ShapeDtypeStruct((pair_count, 2 * lag_pad), jnp.float32),
        compiler_params=pltpu.CompilerParams(
            dimension_semantics=("arbitrary",), vmem_limit_bytes=48 * 1024 * 1024
        ),
        cost_estimate=pl.CostEstimate(
            flops=2 * 2 * pair_count * width * lag_pad,
            transcendentals=0,
            bytes_accessed=4 * width * lag_pad + 4 * pair_count * lag_pad,
        ),
        input_output_aliases={5: 0},
    )(picks, flat, flat, ctab, stab, acc)


def correlate(picks, flat, tables, acc):
    cos_hi, sin_hi, cos_lo, sin_lo = tables
    pair_count = picks.shape[0] // 2
    group_sta = flat.shape[0]
    lag_pad = cos_lo.shape[1]
    width = flat.shape[1] // 2
    hi_rows = FBLOCK // LOW
    assert width % FBLOCK == 0
    blocks = width // FBLOCK
    out = pl.pallas_call(
        table_kernel,
        grid=(blocks,),
        in_specs=[
            pl.BlockSpec((2 * pair_count, group_sta), lambda i: (0, 0)),
            pl.BlockSpec((group_sta, FBLOCK), lambda i: (0, i)),
            pl.BlockSpec((group_sta, FBLOCK), lambda i: (0, i + blocks)),
            pl.BlockSpec((hi_rows, lag_pad), lambda i: (i, 0)),
            pl.BlockSpec((hi_rows, lag_pad), lambda i: (i, 0)),
            pl.BlockSpec((LOW, lag_pad), lambda i: (0, 0)),
            pl.BlockSpec((LOW, lag_pad), lambda i: (0, 0)),
            pl.BlockSpec((pair_count, 2 * lag_pad), lambda i: (0, 0)),
        ],
        out_specs=pl.BlockSpec((pair_count, 2 * lag_pad), lambda i: (0, 0)),
        out_shape=jax.ShapeDtypeStruct((pair_count, 2 * lag_pad), jnp.float32),
        scratch_shapes=[
            pltpu.VMEM((FBLOCK, lag_pad), jnp.bfloat16),
            pltpu.VMEM((FBLOCK, lag_pad), jnp.bfloat16),
        ],
        compiler_params=pltpu.CompilerParams(
            dimension_semantics=("arbitrary",), vmem_limit_bytes=48 * 1024 * 1024
        ),
        cost_estimate=pl.CostEstimate(
            flops=2 * 2 * pair_count * width * lag_pad + 10 * width * lag_pad,
            transcendentals=0,
            bytes_accessed=4 * pair_count * width * 2 + 4 * pair_count * lag_pad,
        ),
        input_output_aliases={7: 0},
    )(picks, flat, flat, cos_hi, sin_hi, cos_lo, sin_lo, acc)
    return out


def local(spectra, stacks, pair_sta, pair_valid, owner, slot):
    total_bins = spectra.shape[2]
    lag_count = stacks.shape[1]
    stack_rows = stacks.shape[0]
    pair_count = pair_sta.shape[1]
    groups = lax.axis_size("grp")
    members = lax.axis_size("sta")
    devices = groups * members
    capacity = max(2, (4 * pair_count + 3 * devices - 1) // (3 * devices))
    group_sta = spectra.shape[0] * members
    sta_ids = lax.iota(jnp.int32, group_sta)[None, :]
    pick0 = (pair_sta[0][:, None] == sta_ids).astype(jnp.bfloat16)
    pick1 = (pair_sta[1][:, None] == sta_ids).astype(jnp.bfloat16)
    picks = jnp.concatenate([pick0, pick1], axis=0)
    assert lag_count % 2 == 1
    side = (lag_count - 1) // 2
    lag_pad = -(-(side + 1) // 128) * 128
    hi_all = angle_table(lax.iota(jnp.int32, total_bins // LOW) * LOW, lag_pad, total_bins)
    lo_all = angle_table(lax.iota(jnp.int32, LOW), lag_pad, total_bins)
    blocks = total_bins // FBLOCK
    assert total_bins % FBLOCK == 0
    lead = max(1, min(blocks - 1, (7 * blocks + 4) // 9))
    bounds = [0, lead * FBLOCK, total_bins] if blocks > 1 else [0, total_bins]
    corr = jnp.zeros((pair_count, 2 * lag_pad), jnp.float32)
    stored = fill_tables((hi_all[0], hi_all[1], lo_all[0], lo_all[1]))
    for c in range(len(bounds) - 1):
        begin, end = bounds[c], bounds[c + 1]
        width = end - begin
        raw = spectra[:, :, begin:end]
        if c:
            raw, _ = lax.optimization_barrier((raw, piece))
        piece = whiten(raw).reshape(spectra.shape[0], 2 * width)
        flat = lax.all_gather(piece, "sta", axis=0, tiled=True)
        if c:
            flat, corr = lax.optimization_barrier((flat, corr))
        corr = correlate_stored(picks, flat, stored, corr, begin)
    even = corr[:, : side + 1]
    odd = corr[:, lag_pad : lag_pad + side + 1]
    corr = jnp.concatenate([(even + odd)[:, :0:-1], even - odd], axis=1)
    corr = corr * jnp.float32(total_bins ** (-0.5)) * pair_valid.astype(jnp.float32)[:, None]
    lag_ext = -(-(lag_count + 1) // 128) * 128
    corr = jnp.concatenate(
        [corr, slot.astype(jnp.float32)[:, None], jnp.zeros((pair_count, lag_ext - lag_count - 1), jnp.float32)],
        axis=1,
    )
    dest = owner[:, 0]
    dest_hot = (dest[:, None] == lax.iota(jnp.int32, devices)[None, :]).astype(jnp.int32)
    before = jnp.cumsum(dest_hot, axis=0) - dest_hot
    position = jnp.sum(before * dest_hot, axis=1)
    flat = dest * capacity + position
    placing = (flat[:, None] == lax.iota(jnp.int32, devices * capacity)[None, :]).astype(
        jnp.float32
    )
    send_rows = jnp.dot(placing.T, corr, precision=lax.Precision.HIGHEST)
    got = lax.all_to_all(
        send_rows.reshape(devices, capacity, corr.shape[1]),
        ("grp", "sta"),
        split_axis=0,
        concat_axis=0,
        tiled=True,
    ).reshape(devices * capacity, corr.shape[1])
    got_rows = got[:, :lag_count]
    got_slots = got[:, lag_count]
    adding = (
        got_slots[None, :] == lax.iota(jnp.int32, stack_rows).astype(jnp.float32)[:, None]
    ).astype(jnp.float32)
    return stacks + jnp.dot(adding, got_rows, precision=lax.Precision.HIGHEST)


def solution(mesh):
    return jax.shard_map(
        local,
        mesh=mesh,
        in_specs=(
            P(("grp", "sta"), None, None),
            P(("grp", "sta"), None),
            P(None, ("grp", "sta")),
            P(("grp", "sta")),
            P(("grp", "sta"), None),
            P(("grp", "sta")),
        ),
        out_specs=P(("grp", "sta"), None),
        check_vma=False,
    )
```

```python
import math

import jax
import jax.numpy as jnp
from jax import lax
from jax.experimental import pallas as pl
from jax.experimental.pallas import tpu as pltpu
from jax.sharding import PartitionSpec as P

BAND = 64


def whiten(spectra):
    shape = spectra.shape
    split = spectra.reshape(shape[0], 2, shape[2] // BAND, BAND)
    power = jnp.mean(split * split, axis=(1, 3), keepdims=True)
    return (split * lax.rsqrt(power + 1e-06)).reshape(shape).astype(jnp.bfloat16)


def angle_table(freqs, lag_pad, total_bins):
    shifts = lax.iota(jnp.int32, lag_pad)
    angle_ids = jnp.mod(freqs[:, None] * shifts[None, :], 2 * total_bins)
    theta = angle_ids.astype(jnp.float32) * jnp.float32(math.pi / total_bins)
    return jnp.cos(theta), jnp.sin(theta)


LOW = 64
FBLOCK = 2048


def table_kernel(pick_ref, g0_ref, g1_ref, chi_ref, shi_ref, clo_ref, slo_ref, acc_ref, out_ref, ctab, stab):
    @pl.when(pl.program_id(0) == 0)
    def _():
        out_ref[...] = acc_ref[...]

    pairs = out_ref.shape[0]
    picks = pick_ref[...]
    rows0 = jnp.dot(picks, g0_ref[...], preferred_element_type=jnp.float32)
    rows1 = jnp.dot(picks, g1_ref[...], preferred_element_type=jnp.float32)
    a0 = rows0[:pairs]
    b0 = rows0[pairs:]
    a1 = rows1[:pairs]
    b1 = rows1[pairs:]
    real = (a0 * b0 + a1 * b1).astype(jnp.bfloat16)
    imag = (a1 * b0 - a0 * b1).astype(jnp.bfloat16)

    def fill(j, carry):
        clo = clo_ref[...]
        slo = slo_ref[...]
        ch = chi_ref[pl.ds(j, 1), :]
        sh = shi_ref[pl.ds(j, 1), :]
        rows = pl.ds(pl.multiple_of(j * LOW, LOW), LOW)
        ctab[rows, :] = (ch * clo - sh * slo).astype(jnp.bfloat16)
        stab[rows, :] = (sh * clo + ch * slo).astype(jnp.bfloat16)
        return carry

    lax.fori_loop(0, FBLOCK // LOW, fill, 0)
    half = ctab.shape[1]
    out_ref[:, :half] += jnp.dot(real, ctab[...], preferred_element_type=jnp.float32)
    out_ref[:, half:] += jnp.dot(imag, stab[...], preferred_element_type=jnp.float32)


def fill_kernel(chi_ref, shi_ref, clo_ref, slo_ref, ctab, stab):
    def fill(j, carry):
        clo = clo_ref[...]
        slo = slo_ref[...]
        ch = chi_ref[pl.ds(j, 1), :]
        sh = shi_ref[pl.ds(j, 1), :]
        rows = pl.ds(pl.multiple_of(j * LOW, LOW), LOW)
        ctab[rows, :] = (ch * clo - sh * slo).astype(jnp.bfloat16)
        stab[rows, :] = (sh * clo + ch * slo).astype(jnp.bfloat16)
        return carry

    lax.fori_loop(0, FBLOCK // LOW, fill, 0)


def stored_kernel(pick_ref, g0_ref, g1_ref, ctab, stab, acc_ref, out_ref):
    @pl.when(pl.program_id(0) == 0)
    def _():
        out_ref[...] = acc_ref[...]

    pairs = out_ref.shape[0]
    picks = pick_ref[...]
    rows0 = jnp.dot(picks, g0_ref[...], preferred_element_type=jnp.float32)
    rows1 = jnp.dot(picks, g1_ref[...], preferred_element_type=jnp.float32)
    a0 = rows0[:pairs]
    b0 = rows0[pairs:]
    a1 = rows1[:pairs]
    b1 = rows1[pairs:]
    real = (a0 * b0 + a1 * b1).astype(jnp.bfloat16)
    imag = (a1 * b0 - a0 * b1).astype(jnp.bfloat16)
    half = ctab.shape[1]
    out_ref[:, :half] += jnp.dot(real, ctab[...], preferred_element_type=jnp.float32)
    out_ref[:, half:] += jnp.dot(imag, stab[...], preferred_element_type=jnp.float32)


def fill_tables(tables):
    cos_hi, sin_hi, cos_lo, sin_lo = tables
    lag_pad = cos_lo.shape[1]
    hi_rows = FBLOCK // LOW
    width = cos_hi.shape[0] * LOW
    blocks = width // FBLOCK
    spec = pl.BlockSpec((FBLOCK, lag_pad), lambda i: (i, 0))
    return pl.pallas_call(
        fill_kernel,
        grid=(blocks,),
        in_specs=[
            pl.BlockSpec((hi_rows, lag_pad), lambda i: (i, 0)),
            pl.BlockSpec((hi_rows, lag_pad), lambda i: (i, 0)),
            pl.BlockSpec((LOW, lag_pad), lambda i: (0, 0)),
            pl.BlockSpec((LOW, lag_pad), lambda i: (0, 0)),
        ],
        out_specs=[spec, spec],
        out_shape=[jax.ShapeDtypeStruct((width, lag_pad), jnp.bfloat16)] * 2,
        compiler_params=pltpu.CompilerParams(
            dimension_semantics=("arbitrary",), vmem_limit_bytes=48 * 1024 * 1024
        ),
        cost_estimate=pl.CostEstimate(
            flops=10 * width * lag_pad, transcendentals=0, bytes_accessed=4 * width * lag_pad
        ),
    )(cos_hi, sin_hi, cos_lo, sin_lo)


def correlate_stored(picks, flat, stored, acc, begin):
    ctab, stab = stored
    pair_count = picks.shape[0] // 2
    group_sta = flat.shape[0]
    lag_pad = ctab.shape[1]
    width = flat.shape[1] // 2
    assert width % FBLOCK == 0 and begin % FBLOCK == 0
    blocks = width // FBLOCK
    skip = begin // FBLOCK
    return pl.pallas_call(
        stored_kernel,
        grid=(blocks,),
        in_specs=[
            pl.BlockSpec((2 * pair_count, group_sta), lambda i: (0, 0)),
            pl.BlockSpec((group_sta, FBLOCK), lambda i: (0, i)),
            pl.BlockSpec((group_sta, FBLOCK), lambda i: (0, i + blocks)),
            pl.BlockSpec((FBLOCK, lag_pad), lambda i: (i + skip, 0)),
            pl.BlockSpec((FBLOCK, lag_pad), lambda i: (i + skip, 0)),
            pl.BlockSpec((pair_count, 2 * lag_pad), lambda i: (0, 0)),
        ],
        out_specs=pl.BlockSpec((pair_count, 2 * lag_pad), lambda i: (0, 0)),
        out_shape=jax.ShapeDtypeStruct((pair_count, 2 * lag_pad), jnp.float32),
        compiler_params=pltpu.CompilerParams(
            dimension_semantics=("arbitrary",), vmem_limit_bytes=48 * 1024 * 1024
        ),
        cost_estimate=pl.CostEstimate(
            flops=2 * 2 * pair_count * width * lag_pad,
            transcendentals=0,
            bytes_accessed=4 * width * lag_pad + 4 * pair_count * lag_pad,
        ),
        input_output_aliases={5: 0},
    )(picks, flat, flat, ctab, stab, acc)


def correlate(picks, flat, tables, acc):
    cos_hi, sin_hi, cos_lo, sin_lo = tables
    pair_count = picks.shape[0] // 2
    group_sta = flat.shape[0]
    lag_pad = cos_lo.shape[1]
    width = flat.shape[1] // 2
    hi_rows = FBLOCK // LOW
    assert width % FBLOCK == 0
    blocks = width // FBLOCK
    out = pl.pallas_call(
        table_kernel,
        grid=(blocks,),
        in_specs=[
            pl.BlockSpec((2 * pair_count, group_sta), lambda i: (0, 0)),
            pl.BlockSpec((group_sta, FBLOCK), lambda i: (0, i)),
            pl.BlockSpec((group_sta, FBLOCK), lambda i: (0, i + blocks)),
            pl.BlockSpec((hi_rows, lag_pad), lambda i: (i, 0)),
            pl.BlockSpec((hi_rows, lag_pad), lambda i: (i, 0)),
            pl.BlockSpec((LOW, lag_pad), lambda i: (0, 0)),
            pl.BlockSpec((LOW, lag_pad), lambda i: (0, 0)),
            pl.BlockSpec((pair_count, 2 * lag_pad), lambda i: (0, 0)),
        ],
        out_specs=pl.BlockSpec((pair_count, 2 * lag_pad), lambda i: (0, 0)),
        out_shape=jax.ShapeDtypeStruct((pair_count, 2 * lag_pad), jnp.float32),
        scratch_shapes=[
            pltpu.VMEM((FBLOCK, lag_pad), jnp.bfloat16),
            pltpu.VMEM((FBLOCK, lag_pad), jnp.bfloat16),
        ],
        compiler_params=pltpu.CompilerParams(
            dimension_semantics=("arbitrary",), vmem_limit_bytes=48 * 1024 * 1024
        ),
        cost_estimate=pl.CostEstimate(
            flops=2 * 2 * pair_count * width * lag_pad + 10 * width * lag_pad,
            transcendentals=0,
            bytes_accessed=4 * pair_count * width * 2 + 4 * pair_count * lag_pad,
        ),
        input_output_aliases={7: 0},
    )(picks, flat, flat, cos_hi, sin_hi, cos_lo, sin_lo, acc)
    return out


def local(spectra, stacks, pair_sta, pair_valid, owner, slot):
    total_bins = spectra.shape[2]
    lag_count = stacks.shape[1]
    stack_rows = stacks.shape[0]
    pair_count = pair_sta.shape[1]
    groups = lax.axis_size("grp")
    members = lax.axis_size("sta")
    devices = groups * members
    capacity = max(2, (4 * pair_count + 3 * devices - 1) // (3 * devices))
    group_sta = spectra.shape[0] * members
    sta_ids = lax.iota(jnp.int32, group_sta)[None, :]
    pick0 = (pair_sta[0][:, None] == sta_ids).astype(jnp.bfloat16)
    pick1 = (pair_sta[1][:, None] == sta_ids).astype(jnp.bfloat16)
    picks = jnp.concatenate([pick0, pick1], axis=0)
    assert lag_count % 2 == 1
    side = (lag_count - 1) // 2
    lag_pad = -(-(side + 1) // 128) * 128
    hi_all = angle_table(lax.iota(jnp.int32, total_bins // LOW) * LOW, lag_pad, total_bins)
    lo_all = angle_table(lax.iota(jnp.int32, LOW), lag_pad, total_bins)
    blocks = total_bins // FBLOCK
    assert total_bins % FBLOCK == 0
    lead = max(1, min(blocks - 1, (2 * blocks + 1) // 3))
    bounds = [0, lead * FBLOCK, total_bins] if blocks > 1 else [0, total_bins]
    corr = jnp.zeros((pair_count, 2 * lag_pad), jnp.float32)
    stored = fill_tables((hi_all[0], hi_all[1], lo_all[0], lo_all[1]))
    for c in range(len(bounds) - 1):
        begin, end = bounds[c], bounds[c + 1]
        width = end - begin
        raw = spectra[:, :, begin:end]
        if c:
            raw, _ = lax.optimization_barrier((raw, piece))
        piece = whiten(raw).reshape(spectra.shape[0], 2 * width)
        if c:
            copies = jnp.broadcast_to(piece[None], (members,) + piece.shape)
            flat = lax.all_to_all(copies, "sta", 0, 0, tiled=True).reshape(group_sta, 2 * width)
        else:
            flat = lax.all_gather(piece, "sta", axis=0, tiled=True)
        if c:
            flat, corr = lax.optimization_barrier((flat, corr))
        corr = correlate_stored(picks, flat, stored, corr, begin)
    even = corr[:, : side + 1]
    odd = corr[:, lag_pad : lag_pad + side + 1]
    corr = jnp.concatenate([(even + odd)[:, :0:-1], even - odd], axis=1)
    corr = corr * jnp.float32(total_bins ** (-0.5)) * pair_valid.astype(jnp.float32)[:, None]
    lag_ext = -(-(lag_count + 1) // 128) * 128
    corr = jnp.concatenate(
        [corr, slot.astype(jnp.float32)[:, None], jnp.zeros((pair_count, lag_ext - lag_count - 1), jnp.float32)],
        axis=1,
    )
    dest = owner[:, 0]
    dest_hot = (dest[:, None] == lax.iota(jnp.int32, devices)[None, :]).astype(jnp.int32)
    before = jnp.cumsum(dest_hot, axis=0) - dest_hot
    position = jnp.sum(before * dest_hot, axis=1)
    flat = dest * capacity + position
    placing = (flat[:, None] == lax.iota(jnp.int32, devices * capacity)[None, :]).astype(
        jnp.float32
    )
    send_rows = jnp.dot(placing.T, corr, precision=lax.Precision.HIGHEST)
    got = lax.all_to_all(
        send_rows.reshape(devices, capacity, corr.shape[1]),
        ("grp", "sta"),
        split_axis=0,
        concat_axis=0,
        tiled=True,
    ).reshape(devices * capacity, corr.shape[1])
    got_rows = got[:, :lag_count]
    got_slots = got[:, lag_count]
    adding = (
        got_slots[None, :] == lax.iota(jnp.int32, stack_rows).astype(jnp.float32)[:, None]
    ).astype(jnp.float32)
    return stacks + jnp.dot(adding, got_rows, precision=lax.Precision.HIGHEST)


def solution(mesh):
    return jax.shard_map(
        local,
        mesh=mesh,
        in_specs=(
            P(("grp", "sta"), None, None),
            P(("grp", "sta"), None),
            P(None, ("grp", "sta")),
            P(("grp", "sta")),
            P(("grp", "sta"), None),
            P(("grp", "sta")),
        ),
        out_specs=P(("grp", "sta"), None),
        check_vma=False,
    )
```

```python
import math

import jax
import jax.numpy as jnp
from jax import lax
from jax.experimental import pallas as pl
from jax.experimental.pallas import tpu as pltpu
from jax.sharding import PartitionSpec as P

BAND = 64


def whiten(spectra):
    shape = spectra.shape
    split = spectra.reshape(shape[0], 2, shape[2] // BAND, BAND)
    power = jnp.mean(split * split, axis=(1, 3), keepdims=True)
    return (split * lax.rsqrt(power + 1e-06)).reshape(shape).astype(jnp.bfloat16)


def angle_table(freqs, lag_pad, total_bins):
    shifts = lax.iota(jnp.int32, lag_pad)
    angle_ids = jnp.mod(freqs[:, None] * shifts[None, :], 2 * total_bins)
    theta = angle_ids.astype(jnp.float32) * jnp.float32(math.pi / total_bins)
    return jnp.cos(theta), jnp.sin(theta)


LOW = 64
FBLOCK = 2048


def table_kernel(pick_ref, g0_ref, g1_ref, chi_ref, shi_ref, clo_ref, slo_ref, acc_ref, out_ref, ctab, stab):
    @pl.when(pl.program_id(0) == 0)
    def _():
        out_ref[...] = acc_ref[...]

    pairs = out_ref.shape[0]
    picks = pick_ref[...]
    rows0 = jnp.dot(picks, g0_ref[...], preferred_element_type=jnp.float32)
    rows1 = jnp.dot(picks, g1_ref[...], preferred_element_type=jnp.float32)
    a0 = rows0[:pairs]
    b0 = rows0[pairs:]
    a1 = rows1[:pairs]
    b1 = rows1[pairs:]
    real = (a0 * b0 + a1 * b1).astype(jnp.bfloat16)
    imag = (a1 * b0 - a0 * b1).astype(jnp.bfloat16)

    def fill(j, carry):
        clo = clo_ref[...]
        slo = slo_ref[...]
        ch = chi_ref[pl.ds(j, 1), :]
        sh = shi_ref[pl.ds(j, 1), :]
        rows = pl.ds(pl.multiple_of(j * LOW, LOW), LOW)
        ctab[rows, :] = (ch * clo - sh * slo).astype(jnp.bfloat16)
        stab[rows, :] = (sh * clo + ch * slo).astype(jnp.bfloat16)
        return carry

    lax.fori_loop(0, FBLOCK // LOW, fill, 0)
    half = ctab.shape[1]
    out_ref[:, :half] += jnp.dot(real, ctab[...], preferred_element_type=jnp.float32)
    out_ref[:, half:] += jnp.dot(imag, stab[...], preferred_element_type=jnp.float32)


def fill_kernel(chi_ref, shi_ref, clo_ref, slo_ref, ctab, stab):
    def fill(j, carry):
        clo = clo_ref[...]
        slo = slo_ref[...]
        ch = chi_ref[pl.ds(j, 1), :]
        sh = shi_ref[pl.ds(j, 1), :]
        rows = pl.ds(pl.multiple_of(j * LOW, LOW), LOW)
        ctab[rows, :] = (ch * clo - sh * slo).astype(jnp.bfloat16)
        stab[rows, :] = (sh * clo + ch * slo).astype(jnp.bfloat16)
        return carry

    lax.fori_loop(0, FBLOCK // LOW, fill, 0)


def stored_kernel(pick_ref, g0_ref, g1_ref, ctab, stab, acc_ref, out_ref):
    @pl.when(pl.program_id(0) == 0)
    def _():
        out_ref[...] = acc_ref[...]

    pairs = out_ref.shape[0]
    picks = pick_ref[...]
    rows0 = jnp.dot(picks, g0_ref[...], preferred_element_type=jnp.float32)
    rows1 = jnp.dot(picks, g1_ref[...], preferred_element_type=jnp.float32)
    a0 = rows0[:pairs]
    b0 = rows0[pairs:]
    a1 = rows1[:pairs]
    b1 = rows1[pairs:]
    real = (a0 * b0 + a1 * b1).astype(jnp.bfloat16)
    imag = (a1 * b0 - a0 * b1).astype(jnp.bfloat16)
    half = ctab.shape[1]
    out_ref[:, :half] += jnp.dot(real, ctab[...], preferred_element_type=jnp.float32)
    out_ref[:, half:] += jnp.dot(imag, stab[...], preferred_element_type=jnp.float32)


def fill_tables(tables):
    cos_hi, sin_hi, cos_lo, sin_lo = tables
    lag_pad = cos_lo.shape[1]
    hi_rows = FBLOCK // LOW
    width = cos_hi.shape[0] * LOW
    blocks = width // FBLOCK
    spec = pl.BlockSpec((FBLOCK, lag_pad), lambda i: (i, 0))
    return pl.pallas_call(
        fill_kernel,
        grid=(blocks,),
        in_specs=[
            pl.BlockSpec((hi_rows, lag_pad), lambda i: (i, 0)),
            pl.BlockSpec((hi_rows, lag_pad), lambda i: (i, 0)),
            pl.BlockSpec((LOW, lag_pad), lambda i: (0, 0)),
            pl.BlockSpec((LOW, lag_pad), lambda i: (0, 0)),
        ],
        out_specs=[spec, spec],
        out_shape=[jax.ShapeDtypeStruct((width, lag_pad), jnp.bfloat16)] * 2,
        compiler_params=pltpu.CompilerParams(
            dimension_semantics=("arbitrary",), vmem_limit_bytes=48 * 1024 * 1024
        ),
        cost_estimate=pl.CostEstimate(
            flops=10 * width * lag_pad, transcendentals=0, bytes_accessed=4 * width * lag_pad
        ),
    )(cos_hi, sin_hi, cos_lo, sin_lo)


def correlate_stored(picks, flat, stored, acc, begin, fblock):
    ctab, stab = stored
    pair_count = picks.shape[0] // 2
    group_sta = flat.shape[0]
    lag_pad = ctab.shape[1]
    width = flat.shape[1] // 2
    assert width % fblock == 0 and begin % fblock == 0
    blocks = width // fblock
    skip = begin // fblock
    return pl.pallas_call(
        stored_kernel,
        grid=(blocks,),
        in_specs=[
            pl.BlockSpec((2 * pair_count, group_sta), lambda i: (0, 0)),
            pl.BlockSpec((group_sta, fblock), lambda i: (0, i)),
            pl.BlockSpec((group_sta, fblock), lambda i: (0, i + blocks)),
            pl.BlockSpec((fblock, lag_pad), lambda i: (i + skip, 0)),
            pl.BlockSpec((fblock, lag_pad), lambda i: (i + skip, 0)),
            pl.BlockSpec((pair_count, 2 * lag_pad), lambda i: (0, 0)),
        ],
        out_specs=pl.BlockSpec((pair_count, 2 * lag_pad), lambda i: (0, 0)),
        out_shape=jax.ShapeDtypeStruct((pair_count, 2 * lag_pad), jnp.float32),
        compiler_params=pltpu.CompilerParams(
            dimension_semantics=("arbitrary",), vmem_limit_bytes=48 * 1024 * 1024
        ),
        cost_estimate=pl.CostEstimate(
            flops=2 * 2 * pair_count * width * lag_pad,
            transcendentals=0,
            bytes_accessed=4 * width * lag_pad + 4 * pair_count * lag_pad,
        ),
        input_output_aliases={5: 0},
    )(picks, flat, flat, ctab, stab, acc)


def correlate(picks, flat, tables, acc):
    cos_hi, sin_hi, cos_lo, sin_lo = tables
    pair_count = picks.shape[0] // 2
    group_sta = flat.shape[0]
    lag_pad = cos_lo.shape[1]
    width = flat.shape[1] // 2
    hi_rows = FBLOCK // LOW
    assert width % FBLOCK == 0
    blocks = width // FBLOCK
    out = pl.pallas_call(
        table_kernel,
        grid=(blocks,),
        in_specs=[
            pl.BlockSpec((2 * pair_count, group_sta), lambda i: (0, 0)),
            pl.BlockSpec((group_sta, FBLOCK), lambda i: (0, i)),
            pl.BlockSpec((group_sta, FBLOCK), lambda i: (0, i + blocks)),
            pl.BlockSpec((hi_rows, lag_pad), lambda i: (i, 0)),
            pl.BlockSpec((hi_rows, lag_pad), lambda i: (i, 0)),
            pl.BlockSpec((LOW, lag_pad), lambda i: (0, 0)),
            pl.BlockSpec((LOW, lag_pad), lambda i: (0, 0)),
            pl.BlockSpec((pair_count, 2 * lag_pad), lambda i: (0, 0)),
        ],
        out_specs=pl.BlockSpec((pair_count, 2 * lag_pad), lambda i: (0, 0)),
        out_shape=jax.ShapeDtypeStruct((pair_count, 2 * lag_pad), jnp.float32),
        scratch_shapes=[
            pltpu.VMEM((FBLOCK, lag_pad), jnp.bfloat16),
            pltpu.VMEM((FBLOCK, lag_pad), jnp.bfloat16),
        ],
        compiler_params=pltpu.CompilerParams(
            dimension_semantics=("arbitrary",), vmem_limit_bytes=48 * 1024 * 1024
        ),
        cost_estimate=pl.CostEstimate(
            flops=2 * 2 * pair_count * width * lag_pad + 10 * width * lag_pad,
            transcendentals=0,
            bytes_accessed=4 * pair_count * width * 2 + 4 * pair_count * lag_pad,
        ),
        input_output_aliases={7: 0},
    )(picks, flat, flat, cos_hi, sin_hi, cos_lo, sin_lo, acc)
    return out


def local(spectra, stacks, pair_sta, pair_valid, owner, slot):
    total_bins = spectra.shape[2]
    lag_count = stacks.shape[1]
    stack_rows = stacks.shape[0]
    pair_count = pair_sta.shape[1]
    groups = lax.axis_size("grp")
    members = lax.axis_size("sta")
    devices = groups * members
    capacity = max(2, (4 * pair_count + 3 * devices - 1) // (3 * devices))
    group_sta = spectra.shape[0] * members
    sta_ids = lax.iota(jnp.int32, group_sta)[None, :]
    pick0 = (pair_sta[0][:, None] == sta_ids).astype(jnp.bfloat16)
    pick1 = (pair_sta[1][:, None] == sta_ids).astype(jnp.bfloat16)
    picks = jnp.concatenate([pick0, pick1], axis=0)
    assert lag_count % 2 == 1
    side = (lag_count - 1) // 2
    lag_pad = -(-(side + 1) // 128) * 128
    hi_all = angle_table(lax.iota(jnp.int32, total_bins // LOW) * LOW, lag_pad, total_bins)
    lo_all = angle_table(lax.iota(jnp.int32, LOW), lag_pad, total_bins)
    blocks = total_bins // FBLOCK
    assert total_bins % FBLOCK == 0
    lead = max(1, min(blocks - 1, (7 * blocks + 4) // 9))
    bounds = [0, lead * FBLOCK, total_bins] if blocks > 1 else [0, total_bins]
    corr = jnp.zeros((pair_count, 2 * lag_pad), jnp.float32)
    stored = fill_tables((hi_all[0], hi_all[1], lo_all[0], lo_all[1]))
    for c in range(len(bounds) - 1):
        begin, end = bounds[c], bounds[c + 1]
        width = end - begin
        raw = spectra[:, :, begin:end]
        if c:
            raw, _ = lax.optimization_barrier((raw, piece))
        piece = whiten(raw).reshape(spectra.shape[0], 2 * width)
        flat = lax.all_gather(piece, "sta", axis=0, tiled=True)
        if c:
            flat, corr = lax.optimization_barrier((flat, corr))
        corr = correlate_stored(picks, flat, stored, corr, begin, FBLOCK if c == 0 else FBLOCK // 2)
    even = corr[:, : side + 1]
    odd = corr[:, lag_pad : lag_pad + side + 1]
    corr = jnp.concatenate([(even + odd)[:, :0:-1], even - odd], axis=1)
    corr = corr * jnp.float32(total_bins ** (-0.5)) * pair_valid.astype(jnp.float32)[:, None]
    lag_ext = -(-(lag_count + 1) // 128) * 128
    corr = jnp.concatenate(
        [corr, slot.astype(jnp.float32)[:, None], jnp.zeros((pair_count, lag_ext - lag_count - 1), jnp.float32)],
        axis=1,
    )
    dest = owner[:, 0]
    dest_hot = (dest[:, None] == lax.iota(jnp.int32, devices)[None, :]).astype(jnp.int32)
    before = jnp.cumsum(dest_hot, axis=0) - dest_hot
    position = jnp.sum(before * dest_hot, axis=1)
    flat = dest * capacity + position
    placing = (flat[:, None] == lax.iota(jnp.int32, devices * capacity)[None, :]).astype(
        jnp.float32
    )
    send_rows = jnp.dot(placing.T, corr, precision=lax.Precision.HIGHEST)
    got = lax.all_to_all(
        send_rows.reshape(devices, capacity, corr.shape[1]),
        ("grp", "sta"),
        split_axis=0,
        concat_axis=0,
        tiled=True,
    ).reshape(devices * capacity, corr.shape[1])
    got_rows = got[:, :lag_count]
    got_slots = got[:, lag_count]
    adding = (
        got_slots[None, :] == lax.iota(jnp.int32, stack_rows).astype(jnp.float32)[:, None]
    ).astype(jnp.float32)
    return stacks + jnp.dot(adding, got_rows, precision=lax.Precision.HIGHEST)


def solution(mesh):
    return jax.shard_map(
        local,
        mesh=mesh,
        in_specs=(
            P(("grp", "sta"), None, None),
            P(("grp", "sta"), None),
            P(None, ("grp", "sta")),
            P(("grp", "sta")),
            P(("grp", "sta"), None),
            P(("grp", "sta")),
        ),
        out_specs=P(("grp", "sta"), None),
        check_vma=False,
    )
```
